128 devices in a mesh: chaos: 8 (over x, y_hi), space: 16 (over y_lo, z, core).
Axes of the slice: x: 4, y: 4 (y_hi: 2, y_lo: 2; y = y_hi * 2 + y_lo), z: 4, core: 2. Of those that a mesh axis runs over, the one named last changes fastest.
Arguments:
- modes: float32 [120, 128, 2048], P('chaos', 'space'), may hold values from -2 to 2
- kl_fields: float32 [8, 128, 2048], P(None, 'space'), may hold values from 0.1 to 1
- triples: int32 [624, 3], replicated, may hold values from 0 to 119, as said below
- ratios: int32 [624, 2], replicated, may hold values from 1 to 12, as said below
- mode_of_slot: int32 [120], replicated, may hold values from 0 to 119, each once
Outputs:
- applied: float32 [120, 128, 2048], P('chaos', 'space')
The draws below stay inside these ranges and needn't reach their ends.
Inputs may be any that keep to these rules, and one draw needn't show every extreme that they name: `triples`: rows are distinct. Modes are the multi-indices of total degree at most 3 in 7 variables. Every mode i has the row (i, i, 0); every other row (i, j, k) has k of 1 or more, and the multi-indices of i and j differ by one in variable k and agree elsewhere; each such pair appears in both orders. `ratios`: column 0 is a positive numerator, column 1 a denominator of 1 to 4. `mode_of_slot`: A permutation.
All inputs are finite; a program needn't handle non-finite values.
Results may differ from the reference program's by a relative error of at most 0.000082.
Values sent between devices are 32-bit elements; how exact they have to be, the bound alone decides.
No kernel may reach another device: no remote copies, remote signals or barrier semaphores. Data moves between devices by JAX's collectives and lax.ppermute only.
A program may use at most 128 MiB of HBM per device.

```python
import math
import jax
import jax.numpy as jnp
import numpy as np
from jax import lax

KL_TERMS = 8
MODES = 120
COLS = 2048
ROWS = 128


def hermite_table():
    variables = KL_TERMS - 1
    combos = [()]
    for position in range(variables):
        combos = [prefix + (degree,) for prefix in combos for degree in range(4) if sum(prefix) + degree <= 3]
    lookup = {}
    for number, combo in enumerate(combos):
        lookup[combo] = number
    entries = []
    for combo in combos:
        entries.append((lookup[combo], lookup[combo], 0, 1))
    for combo in combos:
        if sum(combo) < 3:
            for position in range(variables):
                raised = combo[:position] + (combo[position] + 1,) + combo[position + 1:]
                lower_mode = lookup[combo]
                upper_mode = lookup[raised]
                entries.append((lower_mode, upper_mode, position + 1, combo[position] + 1))
                entries.append((upper_mode, lower_mode, position + 1, 1))
    return np.array(entries, dtype=np.int32)


def hermite_rows(key):
    table = jnp.asarray(hermite_table())
    shuffle = jax.random.permutation(jax.random.fold_in(key, 7), table.shape[0])
    return table[shuffle]


def draw_triples(key, part):
    return hermite_rows(key)[:, :3].astype(jnp.int32)


def draw_ratios(key, part):
    table_rows = hermite_rows(key)
    split_keys = jax.random.split(jax.random.fold_in(key, 13), 2)
    amplitude = jax.random.randint(split_keys[0], (KL_TERMS,), 1, 5).at[1].set(4).at[0].set(1)
    divisor = jax.random.randint(split_keys[1], (KL_TERMS,), 1, 5).at[2].set(4).at[0].set(1)
    numerator = table_rows[:, 3] * amplitude[table_rows[:, 2]]
    denominator = divisor[table_rows[:, 2]]
    return jnp.stack([numerator, denominator], axis=1).astype(jnp.int32)


def level_of(key, shape, cuts, smallest, largest):
    def one(axis_at, blocks):
        heights = jax.random.uniform(jax.random.fold_in(jax.random.fold_in(key, 6), axis_at), (blocks,), jnp.float32, smallest / len(cuts), largest / len(cuts))
        return jnp.repeat(jnp.exp(heights), shape[axis_at] // blocks).reshape((-1,) + (1,) * (len(shape) - axis_at - 1))

    gain = one(*cuts[0])
    for cut in cuts[1:]:
        gain = gain * one(*cut)
    return gain


def normal_values(rng, dims, width, reach, pieces=(), kind=jnp.bfloat16):
    gain = level_of(rng, dims, pieces, -0.22, 0.18) if pieces else 1.0
    values = jax.random.normal(rng, dims, jnp.float32) * width * gain
    return jnp.minimum(jnp.maximum(values, -reach), reach).astype(kind)


def setup_inputs(seed: int = 0) -> dict:
    key_list = jax.random.split(jax.random.key(seed), 6)
    return {
        "modes": normal_values(key_list[0], (MODES, ROWS, COLS), 0.3, 2.0, ((0, 8), (1, 16)), jnp.float32),
        "kl_fields": jnp.clip(jnp.exp(math.log(1.0) - 2.3025851 * jax.random.uniform(key_list[1], (KL_TERMS, ROWS, COLS), jnp.float32) ** level_of(key_list[1], (KL_TERMS, ROWS, COLS), ((1, 16),), -0.2, 0.2)), 0.1, 1.0),
        "triples": draw_triples(jax.random.fold_in(key_list[5], 71), 0),
        "ratios": draw_ratios(jax.random.fold_in(key_list[5], 71), 0),
        "mode_of_slot": jax.random.permutation(key_list[4], MODES).astype(jnp.int32),
    }


def diffuse(values, factor):
    center = values[:, 1:-1, :]
    coef_mid = factor[1:-1, :]
    result = (coef_mid + factor[:-2, :]) * (center - values[:, :-2, :])
    result = result + (coef_mid + factor[2:, :]) * (center - values[:, 2:, :])
    zero_col = jnp.zeros_like(center[:, :, :1])
    left_cell = jnp.concatenate([zero_col, center[:, :, :-1]], axis=2)
    right_cell = jnp.concatenate([center[:, :, 1:], zero_col], axis=2)
    coef_zero = jnp.zeros_like(coef_mid[:, :1])
    coef_left = jnp.concatenate([coef_zero, coef_mid[:, :-1]], axis=1)
    coef_right = jnp.concatenate([coef_mid[:, 1:], coef_zero], axis=1)
    result = result + (coef_mid + coef_left) * (center - left_cell)
    result = result + (coef_mid + coef_right) * (center - right_cell)
    return 0.5 * result


def reference(modes, kl_fields, triples, ratios, mode_of_slot):
    mode_count = modes.shape[0]
    matches = triples[:, :2, None] == mode_of_slot[None, None, :]
    slot_pairs = jnp.sum(jnp.where(matches, jnp.arange(mode_count, dtype=jnp.int32), 0), axis=2).astype(jnp.int32)
    weights = ratios[:, 0].astype(jnp.float32) / ratios[:, 1].astype(jnp.float32)
    padded_modes = jnp.pad(modes, ((0, 0), (1, 1), (0, 0)))
    padded_coef = jnp.pad(kl_fields, ((0, 0), (1, 1), (0, 0)))

    def accumulate(running, triple_item):
        slot_pair, kl_index, weight = triple_item
        one_field = lax.dynamic_slice_in_dim(padded_modes, slot_pair[1], 1, 0)
        factor = lax.dynamic_slice_in_dim(padded_coef, kl_index, 1, 0)[0]
        stencil_image = weight * diffuse(one_field, factor)
        current = lax.dynamic_slice_in_dim(running, slot_pair[0], 1, 0)
        running = lax.dynamic_update_slice_in_dim(running, current + stencil_image, slot_pair[0], 0)
        return running, None

    running, _ = lax.scan(accumulate, jnp.zeros(modes.shape, jnp.float32), (slot_pairs, triples[:, 2], weights))
    return running
```

```python
import jax
import jax.numpy as jnp
from jax import lax
from jax.sharding import PartitionSpec as P


def extended_2(x, sides, width):
    for axis, dim in sides:
        count, length = (lax.axis_size(axis), x.shape[dim])
        up = [(i, (i + 1) % count) for i in range(count - 1)]
        down = [(j, i) for i, j in up]
        last = lax.slice_in_dim(x, length - width, length, axis=dim)
        first = lax.slice_in_dim(x, 0, width, axis=dim)
        before = lax.ppermute(last, axis, up)
        after = lax.ppermute(first, axis, down)
        x = jnp.concatenate([before, x, after], axis=dim)
    return x


def shift_cols(x, direction):
    zero = jnp.zeros_like(x[..., :1])
    if direction > 0:
        return jnp.concatenate([zero, x[..., :-1]], axis=-1)
    return jnp.concatenate([x[..., 1:], zero], axis=-1)


def coupling_table(triples, ratios, mode_of_slot, kl_terms, mode_count):
    matches = triples[:, :2, None] == mode_of_slot[None, None, :]
    slot_pairs = jnp.sum(jnp.where(matches, jnp.arange(mode_count, dtype=jnp.int32), 0), axis=2)
    weights = ratios[:, 0].astype(jnp.float32) / ratios[:, 1].astype(jnp.float32)
    flat_index = (triples[:, 2] * mode_count + slot_pairs[:, 0]) * mode_count + slot_pairs[:, 1]
    coupling = (
        jnp.zeros((kl_terms * mode_count * mode_count,), jnp.float32).at[flat_index].add(weights)
    )
    return coupling.reshape(kl_terms, mode_count, mode_count)


def neighbour_table(local_rows):
    mode_count = local_rows.shape[-1]
    present = local_rows > 0
    first = jnp.argmax(present, axis=-1).astype(jnp.int32)
    last = (mode_count - 1 - jnp.argmax(present[..., ::-1], axis=-1)).astype(jnp.int32)
    w_first = jnp.take_along_axis(local_rows, first[..., None], axis=-1)[..., 0]
    w_last = jnp.take_along_axis(local_rows, last[..., None], axis=-1)[..., 0]
    w_last = jnp.where(last == first, jnp.zeros_like(w_last), w_last)
    return first, last, w_first, w_last


def local(modes, kl_fields, triples, ratios, mode_of_slot):
    groups = lax.axis_size("chaos")
    own_modes = modes.shape[0]
    mode_count = own_modes * groups
    kl_terms = kl_fields.shape[0]
    first_slot = lax.axis_index("chaos") * own_modes
    coupling = coupling_table(triples, ratios, mode_of_slot, kl_terms, mode_count)
    local_rows = lax.dynamic_slice_in_dim(coupling, first_slot, own_modes, 1)
    first, last, w_first, w_last = neighbour_table(local_rows)

    joined = jnp.concatenate([modes, kl_fields], axis=0)
    padded = extended_2(joined, (("space", 1),), 1)
    source = padded[:own_modes]
    coef = padded[own_modes:]
    every = lax.all_gather(source, "chaos", axis=0, tiled=True)

    a_c = coef[:, 1:-1]
    c_up = (a_c + coef[:, :-2])[:, None]
    c_dn = (a_c + coef[:, 2:])[:, None]
    c_lf = (a_c + shift_cols(a_c, 1))[:, None]
    c_rt = (a_c + shift_cols(a_c, -1))[:, None]

    g_first = jnp.take(every, first.reshape(-1), axis=0).reshape((kl_terms, own_modes) + every.shape[1:])
    g_last = jnp.take(every, last.reshape(-1), axis=0).reshape((kl_terms, own_modes) + every.shape[1:])
    mixed = w_first[:, :, None, None] * g_first + w_last[:, :, None, None] * g_last
    center = mixed[:, :, 1:-1]
    result = c_up * (center - mixed[:, :, :-2])
    result = result + c_dn * (center - mixed[:, :, 2:])
    result = result + c_lf * (center - shift_cols(center, 1))
    result = result + c_rt * (center - shift_cols(center, -1))
    return 0.5 * jnp.sum(result, axis=0)


def solution(mesh):
    return jax.shard_map(
        local,
        mesh=mesh,
        in_specs=(P("chaos", "space", None), P(None, "space", None), P(), P(), P()),
        out_specs=P("chaos", "space", None),
        check_vma=False,
    )
```

```python
import jax
import jax.numpy as jnp
from jax import lax
from jax.sharding import PartitionSpec as P


def extended_2(x, sides, width):
    for axis, dim in sides:
        count, length = (lax.axis_size(axis), x.shape[dim])
        up = [(i, (i + 1) % count) for i in range(count - 1)]
        down = [(j, i) for i, j in up]
        last = lax.slice_in_dim(x, length - width, length, axis=dim)
        first = lax.slice_in_dim(x, 0, width, axis=dim)
        before = lax.ppermute(last, axis, up)
        after = lax.ppermute(first, axis, down)
        x = jnp.concatenate([before, x, after], axis=dim)
    return x


def shift_cols(x, direction):
    zero = jnp.zeros_like(x[..., :1])
    if direction > 0:
        return jnp.concatenate([zero, x[..., :-1]], axis=-1)
    return jnp.concatenate([x[..., 1:], zero], axis=-1)


def coupling_table(triples, ratios, mode_of_slot, kl_terms, mode_count):
    matches = triples[:, :2, None] == mode_of_slot[None, None, :]
    slot_pairs = jnp.sum(jnp.where(matches, jnp.arange(mode_count, dtype=jnp.int32), 0), axis=2)
    weights = ratios[:, 0].astype(jnp.float32) / ratios[:, 1].astype(jnp.float32)
    flat_index = (triples[:, 2] * mode_count + slot_pairs[:, 0]) * mode_count + slot_pairs[:, 1]
    coupling = (
        jnp.zeros((kl_terms * mode_count * mode_count,), jnp.float32).at[flat_index].add(weights)
    )
    return coupling.reshape(kl_terms, mode_count, mode_count)


def neighbour_table(local_rows):
    mode_count = local_rows.shape[-1]
    present = local_rows > 0
    first = jnp.argmax(present, axis=-1).astype(jnp.int32)
    last = (mode_count - 1 - jnp.argmax(present[..., ::-1], axis=-1)).astype(jnp.int32)
    w_first = jnp.take_along_axis(local_rows, first[..., None], axis=-1)[..., 0]
    w_last = jnp.take_along_axis(local_rows, last[..., None], axis=-1)[..., 0]
    w_last = jnp.where(last == first, jnp.zeros_like(w_last), w_last)
    return first, last, w_first, w_last


def shifted(x, step):
    count = lax.axis_size("chaos")
    return lax.ppermute(x, "chaos", [(c, (c + step) % count) for c in range(count)])


def ring_gather(block):
    count = lax.axis_size("chaos")
    me = lax.axis_index("chaos")
    half = block.shape[-1] // 2
    partner = lax.ppermute(block, "chaos", [(c, c ^ 1) for c in range(count)])
    pieces = []
    owners = []
    for base, origin in ((block, me), (partner, me ^ 1)):
        from_left = shifted(base, 2)
        from_right = shifted(base, -2)
        far = jnp.concatenate(
            [shifted(from_left[..., :half], 2), shifted(from_right[..., half:], -2)], axis=-1
        )
        pieces += [base, from_left, from_right, far]
        owners += [origin, (origin - 2) % count, (origin + 2) % count, (origin + 4) % count]
    return jnp.concatenate(pieces, axis=0), jnp.stack(owners).astype(jnp.int32)


def local(modes, kl_fields, triples, ratios, mode_of_slot):
    groups = lax.axis_size("chaos")
    own_modes = modes.shape[0]
    mode_count = own_modes * groups
    kl_terms = kl_fields.shape[0]
    first_slot = lax.axis_index("chaos") * own_modes
    coupling = coupling_table(triples, ratios, mode_of_slot, kl_terms, mode_count)
    local_rows = lax.dynamic_slice_in_dim(coupling, first_slot, own_modes, 1)
    first, last, w_first, w_last = neighbour_table(local_rows)

    joined = jnp.concatenate([modes, kl_fields], axis=0)
    padded = extended_2(joined, (("space", 1),), 1)
    source = padded[:own_modes]
    coef = padded[own_modes:]
    every, order = ring_gather(source)
    owner = jnp.arange(mode_count, dtype=jnp.int32) // own_modes
    position = jnp.argmax(order[None, :] == owner[:, None], axis=1).astype(jnp.int32)
    place = position * own_modes + jnp.arange(mode_count, dtype=jnp.int32) % own_modes
    first = place[first]
    last = place[last]

    a_c = coef[:, 1:-1]
    c_up = (a_c + coef[:, :-2])[:, None]
    c_dn = (a_c + coef[:, 2:])[:, None]
    c_lf = (a_c + shift_cols(a_c, 1))[:, None]
    c_rt = (a_c + shift_cols(a_c, -1))[:, None]

    g_first = jnp.take(every, first.reshape(-1), axis=0).reshape((kl_terms, own_modes) + every.shape[1:])
    g_last = jnp.take(every, last.reshape(-1), axis=0).reshape((kl_terms, own_modes) + every.shape[1:])
    mixed = w_first[:, :, None, None] * g_first + w_last[:, :, None, None] * g_last
    center = mixed[:, :, 1:-1]
    result = c_up * (center - mixed[:, :, :-2])
    result = result + c_dn * (center - mixed[:, :, 2:])
    result = result + c_lf * (center - shift_cols(center, 1))
    result = result + c_rt * (center - shift_cols(center, -1))
    return 0.5 * jnp.sum(result, axis=0)


def solution(mesh):
    return jax.shard_map(
        local,
        mesh=mesh,
        in_specs=(P("chaos", "space", None), P(None, "space", None), P(), P(), P()),
        out_specs=P("chaos", "space", None),
        check_vma=False,
    )
```

```python
import jax
import jax.numpy as jnp
from jax import lax
from jax.experimental import pallas as pl
from jax.experimental.pallas import tpu as pltpu
from jax.sharding import PartitionSpec as P


def extended_2(x, sides, width):
    for axis, dim in sides:
        count, length = (lax.axis_size(axis), x.shape[dim])
        up = [(i, (i + 1) % count) for i in range(count - 1)]
        down = [(j, i) for i, j in up]
        last = lax.slice_in_dim(x, length - width, length, axis=dim)
        first = lax.slice_in_dim(x, 0, width, axis=dim)
        before = lax.ppermute(last, axis, up)
        after = lax.ppermute(first, axis, down)
        x = jnp.concatenate([before, x, after], axis=dim)
    return x


def shift_cols(x, direction):
    zero = jnp.zeros_like(x[..., :1])
    if direction > 0:
        return jnp.concatenate([zero, x[..., :-1]], axis=-1)
    return jnp.concatenate([x[..., 1:], zero], axis=-1)


def coupling_table(triples, ratios, mode_of_slot, kl_terms, mode_count):
    matches = triples[:, :2, None] == mode_of_slot[None, None, :]
    slot_pairs = jnp.sum(jnp.where(matches, jnp.arange(mode_count, dtype=jnp.int32), 0), axis=2)
    weights = ratios[:, 0].astype(jnp.float32) / ratios[:, 1].astype(jnp.float32)
    flat_index = (triples[:, 2] * mode_count + slot_pairs[:, 0]) * mode_count + slot_pairs[:, 1]
    coupling = (
        jnp.zeros((kl_terms * mode_count * mode_count,), jnp.float32).at[flat_index].add(weights)
    )
    return coupling.reshape(kl_terms, mode_count, mode_count)


def neighbour_table(local_rows):
    mode_count = local_rows.shape[-1]
    present = local_rows > 0
    first = jnp.argmax(present, axis=-1).astype(jnp.int32)
    last = (mode_count - 1 - jnp.argmax(present[..., ::-1], axis=-1)).astype(jnp.int32)
    w_first = jnp.take_along_axis(local_rows, first[..., None], axis=-1)[..., 0]
    w_last = jnp.take_along_axis(local_rows, last[..., None], axis=-1)[..., 0]
    w_last = jnp.where(last == first, jnp.zeros_like(w_last), w_last)
    return first, last, w_first, w_last


def shifted(x, step):
    count = lax.axis_size("chaos")
    return lax.ppermute(x, "chaos", [(c, (c + step) % count) for c in range(count)])


def ring_gather(block):
    count = lax.axis_size("chaos")
    me = lax.axis_index("chaos")
    half = block.shape[-1] // 2
    partner = lax.ppermute(block, "chaos", [(c, c ^ 1) for c in range(count)])
    pieces = []
    owners = []
    for base, origin in ((block, me), (partner, me ^ 1)):
        from_left = shifted(base, 2)
        from_right = shifted(base, -2)
        far = jnp.concatenate(
            [shifted(from_left[..., :half], 2), shifted(from_right[..., half:], -2)], axis=-1
        )
        pieces += [base, from_left, from_right, far]
        owners += [origin, (origin - 2) % count, (origin + 2) % count, (origin + 4) % count]
    return jnp.concatenate(pieces, axis=0), jnp.stack(owners).astype(jnp.int32)


def local(modes, kl_fields, triples, ratios, mode_of_slot):
    groups = lax.axis_size("chaos")
    own_modes = modes.shape[0]
    mode_count = own_modes * groups
    kl_terms = kl_fields.shape[0]
    first_slot = lax.axis_index("chaos") * own_modes
    coupling = coupling_table(triples, ratios, mode_of_slot, kl_terms, mode_count)
    local_rows = lax.dynamic_slice_in_dim(coupling, first_slot, own_modes, 1)
    first, last, w_first, w_last = neighbour_table(local_rows)

    joined = jnp.concatenate([modes, kl_fields], axis=0)
    padded = extended_2(joined, (("space", 1),), 1)
    source = padded[:own_modes]
    coef = padded[own_modes:]
    every, order = ring_gather(source)
    owner = jnp.arange(mode_count, dtype=jnp.int32) // own_modes
    position = jnp.argmax(order[None, :] == owner[:, None], axis=1).astype(jnp.int32)
    place = position * own_modes + jnp.arange(mode_count, dtype=jnp.int32) % own_modes
    first = place[first]
    last = place[last]

    weights = jnp.stack([w_first, w_last], axis=-1).transpose(1, 0, 2).reshape(own_modes, 2 * kl_terms)
    partners = jnp.stack([first, last], axis=-1).transpose(1, 0, 2).reshape(own_modes, 2 * kl_terms)
    return stencil_apply(every, edge_coefficients(coef), partners, weights)


def edge_coefficients(coef):
    a_c = coef[:, 1:-1]
    c_up = 0.5 * (a_c + coef[:, :-2])
    c_dn = 0.5 * (a_c + coef[:, 2:])
    c_lf = 0.5 * (a_c + shift_cols(a_c, 1))
    c_rt = 0.5 * (a_c + shift_cols(a_c, -1))
    total = (c_up + c_dn) + (c_lf + c_rt)
    column = lax.broadcasted_iota(jnp.int32, a_c.shape, 2)
    n_lf = jnp.where(column == 0, 0.0, c_lf)
    n_rt = jnp.where(column == a_c.shape[2] - 1, 0.0, c_rt)
    return jnp.stack([total, c_up, c_dn, n_lf, n_rt], axis=0)


def stencil_kernel(partners, weights, every, edges, out):
    slot = pl.program_id(0)
    kl_terms = edges.shape[1]
    rows = out.shape[1]
    cols = out.shape[2]
    acc = jnp.zeros((rows, cols), jnp.float32)
    for k in range(kl_terms):
        j0 = partners[slot, 2 * k]
        j1 = partners[slot, 2 * k + 1]
        w0 = weights[slot, 2 * k]
        w1 = weights[slot, 2 * k + 1]

        def window(offset):
            return w0 * every[j0, pl.ds(offset, rows), :] + w1 * every[j1, pl.ds(offset, rows), :]

        center = window(1)
        up = window(0)
        dn = window(2)
        lf = pltpu.roll(center, 1, 1)
        rt = pltpu.roll(center, cols - 1, 1)
        term = edges[0, k] * center - edges[1, k] * up
        term = term - edges[2, k] * dn
        term = term - edges[3, k] * lf
        term = term - edges[4, k] * rt
        acc = acc + term
    out[0] = acc


def stencil_apply(every, edges, partners, weights):
    own_modes = partners.shape[0]
    rows = edges.shape[2]
    cols = edges.shape[3]
    return pl.pallas_call(
        stencil_kernel,
        out_shape=jax.ShapeDtypeStruct((own_modes, rows, cols), jnp.float32),
        grid_spec=pltpu.PrefetchScalarGridSpec(
            num_scalar_prefetch=1,
            grid=(own_modes,),
            in_specs=[
                pl.BlockSpec(memory_space=pltpu.SMEM),
                pl.BlockSpec(memory_space=pltpu.VMEM),
                pl.BlockSpec(memory_space=pltpu.VMEM),
            ],
            out_specs=pl.BlockSpec((1, rows, cols), lambda i, p: (i, 0, 0)),
        ),
        compiler_params=pltpu.CompilerParams(
            dimension_semantics=("arbitrary",), vmem_limit_bytes=48 * 1024 * 1024
        ),
    )(partners, weights, every, edges)


def solution(mesh):
    return jax.shard_map(
        local,
        mesh=mesh,
        in_specs=(P("chaos", "space", None), P(None, "space", None), P(), P(), P()),
        out_specs=P("chaos", "space", None),
        check_vma=False,
    )
```

```python
import jax
import jax.numpy as jnp
from jax import lax
from jax.experimental import pallas as pl
from jax.experimental.pallas import tpu as pltpu
from jax.sharding import PartitionSpec as P


def extended_2(x, sides, width):
    for axis, dim in sides:
        count, length = (lax.axis_size(axis), x.shape[dim])
        up = [(i, (i + 1) % count) for i in range(count - 1)]
        down = [(j, i) for i, j in up]
        last = lax.slice_in_dim(x, length - width, length, axis=dim)
        first = lax.slice_in_dim(x, 0, width, axis=dim)
        before = lax.ppermute(last, axis, up)
        after = lax.ppermute(first, axis, down)
        x = jnp.concatenate([before, x, after], axis=dim)
    return x


def shift_cols(x, direction):
    zero = jnp.zeros_like(x[..., :1])
    if direction > 0:
        return jnp.concatenate([zero, x[..., :-1]], axis=-1)
    return jnp.concatenate([x[..., 1:], zero], axis=-1)


def coupling_table(triples, ratios, mode_of_slot, kl_terms, mode_count):
    matches = triples[:, :2, None] == mode_of_slot[None, None, :]
    slot_pairs = jnp.sum(jnp.where(matches, jnp.arange(mode_count, dtype=jnp.int32), 0), axis=2)
    weights = ratios[:, 0].astype(jnp.float32) / ratios[:, 1].astype(jnp.float32)
    flat_index = (triples[:, 2] * mode_count + slot_pairs[:, 0]) * mode_count + slot_pairs[:, 1]
    coupling = (
        jnp.zeros((kl_terms * mode_count * mode_count,), jnp.float32).at[flat_index].add(weights)
    )
    return coupling.reshape(kl_terms, mode_count, mode_count)


def neighbour_table(local_rows):
    mode_count = local_rows.shape[-1]
    present = local_rows > 0
    first = jnp.argmax(present, axis=-1).astype(jnp.int32)
    last = (mode_count - 1 - jnp.argmax(present[..., ::-1], axis=-1)).astype(jnp.int32)
    w_first = jnp.take_along_axis(local_rows, first[..., None], axis=-1)[..., 0]
    w_last = jnp.take_along_axis(local_rows, last[..., None], axis=-1)[..., 0]
    w_last = jnp.where(last == first, jnp.zeros_like(w_last), w_last)
    return first, last, w_first, w_last


def shifted(x, step):
    count = lax.axis_size("chaos")
    return lax.ppermute(x, "chaos", [(c, (c + step) % count) for c in range(count)])


def ring_gather(block):
    count = lax.axis_size("chaos")
    me = lax.axis_index("chaos")
    half = block.shape[-1] // 2
    partner = lax.ppermute(block, "chaos", [(c, c ^ 1) for c in range(count)])
    pieces = []
    owners = []
    for base, origin in ((block, me), (partner, me ^ 1)):
        from_left = shifted(base, 2)
        from_right = shifted(base, -2)
        far = jnp.concatenate(
            [shifted(from_left[..., :half], 2), shifted(from_right[..., half:], -2)], axis=-1
        )
        pieces += [base, from_left, from_right, far]
        owners += [origin, (origin - 2) % count, (origin + 2) % count, (origin + 4) % count]
    return jnp.concatenate(pieces, axis=0), jnp.stack(owners).astype(jnp.int32)


def space_halo(edge_last, edge_first):
    count = lax.axis_size("space")
    up = [(i, i + 1) for i in range(count - 1)]
    down = [(i + 1, i) for i in range(count - 1)]
    return lax.ppermute(edge_last, "space", up), lax.ppermute(edge_first, "space", down)


def local(modes, kl_fields, triples, ratios, mode_of_slot):
    groups = lax.axis_size("chaos")
    own_modes = modes.shape[0]
    mode_count = own_modes * groups
    kl_terms = kl_fields.shape[0]
    rows = modes.shape[1]
    every, order = ring_gather(modes)

    first_slot = lax.axis_index("chaos") * own_modes
    coupling = coupling_table(triples, ratios, mode_of_slot, kl_terms, mode_count)
    local_rows = lax.dynamic_slice_in_dim(coupling, first_slot, own_modes, 1)
    first, last, w_first, w_last = neighbour_table(local_rows)
    owner = jnp.arange(mode_count, dtype=jnp.int32) // own_modes
    position = jnp.argmax(order[None, :] == owner[:, None], axis=1).astype(jnp.int32)
    place = position * own_modes + jnp.arange(mode_count, dtype=jnp.int32) % own_modes
    first = place[first]
    last = place[last]
    weights = jnp.stack([w_first, w_last], axis=-1).transpose(1, 0, 2).reshape(own_modes, 2 * kl_terms)
    partners = jnp.stack([first, last], axis=-1).transpose(1, 0, 2).reshape(own_modes, 2 * kl_terms)

    above, below = space_halo(kl_fields[:, rows - 1:], kl_fields[:, :1])
    coef = jnp.concatenate([above, kl_fields, below], axis=1)
    edges, c_top, c_bottom = edge_coefficients(coef)
    applied = stencil_apply(every, edges, partners, weights)

    halo_above, halo_below = space_halo(every[:, rows - 1], every[:, 0])
    pick_w = weights.reshape(own_modes, kl_terms, 2, 1)
    mixed_above = jnp.sum(jnp.take(halo_above, partners, axis=0).reshape(own_modes, kl_terms, 2, -1) * pick_w, axis=2)
    mixed_below = jnp.sum(jnp.take(halo_below, partners, axis=0).reshape(own_modes, kl_terms, 2, -1) * pick_w, axis=2)
    fix_top = jnp.sum(c_top[None] * mixed_above, axis=1)
    fix_bottom = jnp.sum(c_bottom[None] * mixed_below, axis=1)
    applied = applied.at[:, 0].add(-fix_top)
    applied = applied.at[:, rows - 1].add(-fix_bottom)
    return applied


def edge_coefficients(coef):
    a_c = coef[:, 1:-1]
    c_up = 0.5 * (a_c + coef[:, :-2])
    c_dn = 0.5 * (a_c + coef[:, 2:])
    c_lf = 0.5 * (a_c + shift_cols(a_c, 1))
    c_rt = 0.5 * (a_c + shift_cols(a_c, -1))
    total = (c_up + c_dn) + (c_lf + c_rt)
    column = lax.broadcasted_iota(jnp.int32, a_c.shape, 2)
    row = lax.broadcasted_iota(jnp.int32, a_c.shape, 1)
    n_up = jnp.where(row == 0, 0.0, c_up)
    n_dn = jnp.where(row == a_c.shape[1] - 1, 0.0, c_dn)
    n_lf = jnp.where(column == 0, 0.0, c_lf)
    n_rt = jnp.where(column == a_c.shape[2] - 1, 0.0, c_rt)
    edges = jnp.stack([total, n_up, n_dn, n_lf, n_rt], axis=0)
    return edges, c_up[:, 0], c_dn[:, -1]


def stencil_kernel(partners, weights, every, edges, out):
    slot = pl.program_id(0)
    kl_terms = edges.shape[1]
    rows = out.shape[1]
    cols = out.shape[2]
    acc = jnp.zeros((rows, cols), jnp.float32)
    for k in range(kl_terms):
        j0 = partners[slot, 2 * k]
        j1 = partners[slot, 2 * k + 1]
        w0 = weights[slot, 2 * k]
        w1 = weights[slot, 2 * k + 1]
        center = w0 * every[j0] + w1 * every[j1]
        up = pltpu.roll(center, 1, 0)
        dn = pltpu.roll(center, rows - 1, 0)
        lf = pltpu.roll(center, 1, 1)
        rt = pltpu.roll(center, cols - 1, 1)
        term = edges[0, k] * center - edges[1, k] * up
        term = term - edges[2, k] * dn
        term = term - edges[3, k] * lf
        term = term - edges[4, k] * rt
        acc = acc + term
    out[0] = acc


def stencil_apply(every, edges, partners, weights):
    own_modes = partners.shape[0]
    rows = edges.shape[2]
    cols = edges.shape[3]
    return pl.pallas_call(
        stencil_kernel,
        out_shape=jax.ShapeDtypeStruct((own_modes, rows, cols), jnp.float32),
        grid_spec=pltpu.PrefetchScalarGridSpec(
            num_scalar_prefetch=1,
            grid=(own_modes,),
            in_specs=[
                pl.BlockSpec(memory_space=pltpu.SMEM),
                pl.BlockSpec(memory_space=pltpu.VMEM),
                pl.BlockSpec(memory_space=pltpu.VMEM),
            ],
            out_specs=pl.BlockSpec((1, rows, cols), lambda i, p: (i, 0, 0)),
        ),
        compiler_params=pltpu.CompilerParams(
            dimension_semantics=("arbitrary",), vmem_limit_bytes=48 * 1024 * 1024
        ),
    )(partners, weights, every, edges)


def solution(mesh):
    return jax.shard_map(
        local,
        mesh=mesh,
        in_specs=(P("chaos", "space", None), P(None, "space", None), P(), P(), P()),
        out_specs=P("chaos", "space", None),
        check_vma=False,
    )
```

```python
import jax
import jax.numpy as jnp
from jax import lax
from jax.experimental import pallas as pl
from jax.experimental.pallas import tpu as pltpu
from jax.sharding import PartitionSpec as P


def extended_2(x, sides, width):
    for axis, dim in sides:
        count, length = (lax.axis_size(axis), x.shape[dim])
        up = [(i, (i + 1) % count) for i in range(count - 1)]
        down = [(j, i) for i, j in up]
        last = lax.slice_in_dim(x, length - width, length, axis=dim)
        first = lax.slice_in_dim(x, 0, width, axis=dim)
        before = lax.ppermute(last, axis, up)
        after = lax.ppermute(first, axis, down)
        x = jnp.concatenate([before, x, after], axis=dim)
    return x


def shift_cols(x, direction):
    zero = jnp.zeros_like(x[..., :1])
    if direction > 0:
        return jnp.concatenate([zero, x[..., :-1]], axis=-1)
    return jnp.concatenate([x[..., 1:], zero], axis=-1)


def coupling_table(triples, ratios, mode_of_slot, kl_terms, mode_count):
    matches = triples[:, :2, None] == mode_of_slot[None, None, :]
    slot_pairs = jnp.sum(jnp.where(matches, jnp.arange(mode_count, dtype=jnp.int32), 0), axis=2)
    weights = ratios[:, 0].astype(jnp.float32) / ratios[:, 1].astype(jnp.float32)
    flat_index = (triples[:, 2] * mode_count + slot_pairs[:, 0]) * mode_count + slot_pairs[:, 1]
    coupling = (
        jnp.zeros((kl_terms * mode_count * mode_count,), jnp.float32).at[flat_index].add(weights)
    )
    return coupling.reshape(kl_terms, mode_count, mode_count)


def neighbour_table(local_rows):
    mode_count = local_rows.shape[-1]
    present = local_rows > 0
    first = jnp.argmax(present, axis=-1).astype(jnp.int32)
    last = (mode_count - 1 - jnp.argmax(present[..., ::-1], axis=-1)).astype(jnp.int32)
    w_first = jnp.take_along_axis(local_rows, first[..., None], axis=-1)[..., 0]
    w_last = jnp.take_along_axis(local_rows, last[..., None], axis=-1)[..., 0]
    w_last = jnp.where(last == first, jnp.zeros_like(w_last), w_last)
    return first, last, w_first, w_last


def shifted(x, step):
    count = lax.axis_size("chaos")
    return lax.ppermute(x, "chaos", [(c, (c + step) % count) for c in range(count)])


def ring_gather(block):
    count = lax.axis_size("chaos")
    me = lax.axis_index("chaos")
    half = block.shape[-1] // 2
    partner = lax.ppermute(block, "chaos", [(c, c ^ 1) for c in range(count)])
    pieces = []
    owners = []
    for base, origin in ((block, me), (partner, me ^ 1)):
        from_left = shifted(base, 2)
        from_right = shifted(base, -2)
        far = jnp.concatenate(
            [shifted(from_left[..., :half], 2), shifted(from_right[..., half:], -2)], axis=-1
        )
        pieces += [base, from_left, from_right, far]
        owners += [origin, (origin - 2) % count, (origin + 2) % count, (origin + 4) % count]
    return jnp.concatenate(pieces, axis=0), jnp.stack(owners).astype(jnp.int32)


def space_halo(edge_last, edge_first):
    count = lax.axis_size("space")
    up = [(i, i + 1) for i in range(count - 1)]
    down = [(i + 1, i) for i in range(count - 1)]
    return lax.ppermute(edge_last, "space", up), lax.ppermute(edge_first, "space", down)


def local(modes, kl_fields, triples, ratios, mode_of_slot):
    groups = lax.axis_size("chaos")
    own_modes = modes.shape[0]
    mode_count = own_modes * groups
    kl_terms = kl_fields.shape[0]
    rows = modes.shape[1]
    every, order = ring_gather(modes)

    first_slot = lax.axis_index("chaos") * own_modes
    coupling = coupling_table(triples, ratios, mode_of_slot, kl_terms, mode_count)
    local_rows = lax.dynamic_slice_in_dim(coupling, first_slot, own_modes, 1)
    first, last, w_first, w_last = neighbour_table(local_rows)
    owner = jnp.arange(mode_count, dtype=jnp.int32) // own_modes
    position = jnp.argmax(order[None, :] == owner[:, None], axis=1).astype(jnp.int32)
    place = position * own_modes + jnp.arange(mode_count, dtype=jnp.int32) % own_modes
    first = place[first]
    last = place[last]
    weights = jnp.stack([w_first, w_last], axis=-1).transpose(1, 0, 2).reshape(own_modes, 2 * kl_terms)
    partners = jnp.stack([first, last], axis=-1).transpose(1, 0, 2).reshape(own_modes, 2 * kl_terms)

    above, below = space_halo(kl_fields[:, rows - 1:], kl_fields[:, :1])
    coef = jnp.concatenate([above, kl_fields, below], axis=1)
    applied = stencil_apply(every, coef, partners, weights)

    halo_above, halo_below = space_halo(every[:, rows - 1:], every[:, :1])
    halo = jnp.concatenate([halo_above, halo_below], axis=1)
    c_rim = 0.5 * jnp.concatenate([coef[:, 1:2] + coef[:, :1], coef[:, rows:rows + 1] + coef[:, rows + 1:]], axis=1)
    return rim_apply(applied, halo, c_rim, partners, weights)


def stencil_kernel(partners, weights, every, coef, out, edges):
    slot = pl.program_id(0)
    kl_terms = coef.shape[0]
    rows = out.shape[1]
    cols = out.shape[2]

    @pl.when(slot == 0)
    def _():
        row = lax.broadcasted_iota(jnp.int32, (rows, cols), 0)
        column = lax.broadcasted_iota(jnp.int32, (rows, cols), 1)
        zero = jnp.zeros((rows, cols), jnp.float32)
        for k in range(kl_terms):
            a_c = coef[k, pl.ds(1, rows), :]
            c_up = 0.5 * (a_c + coef[k, pl.ds(0, rows), :])
            c_dn = 0.5 * (a_c + coef[k, pl.ds(2, rows), :])
            c_lf = 0.5 * (a_c + jnp.where(column == 0, zero, pltpu.roll(a_c, 1, 1)))
            c_rt = 0.5 * (a_c + jnp.where(column == cols - 1, zero, pltpu.roll(a_c, cols - 1, 1)))
            edges[0, k] = (c_up + c_dn) + (c_lf + c_rt)
            edges[1, k] = jnp.where(row == 0, zero, c_up)
            edges[2, k] = jnp.where(row == rows - 1, zero, c_dn)
            edges[3, k] = jnp.where(column == 0, zero, c_lf)
            edges[4, k] = jnp.where(column == cols - 1, zero, c_rt)

    acc = jnp.zeros((rows, cols), jnp.float32)
    for k in range(kl_terms):
        j0 = partners[slot, 2 * k]
        j1 = partners[slot, 2 * k + 1]
        w0 = weights[slot, 2 * k]
        w1 = weights[slot, 2 * k + 1]
        center = w0 * every[j0] + w1 * every[j1]
        up = pltpu.roll(center, 1, 0)
        dn = pltpu.roll(center, rows - 1, 0)
        lf = pltpu.roll(center, 1, 1)
        rt = pltpu.roll(center, cols - 1, 1)
        term = edges[0, k] * center - edges[1, k] * up
        term = term - edges[2, k] * dn
        term = term - edges[3, k] * lf
        term = term - edges[4, k] * rt
        acc = acc + term
    out[0] = acc


def stencil_apply(every, coef, partners, weights):
    own_modes = partners.shape[0]
    kl_terms = coef.shape[0]
    rows = every.shape[1]
    cols = every.shape[2]
    return pl.pallas_call(
        stencil_kernel,
        out_shape=jax.ShapeDtypeStruct((own_modes, rows, cols), jnp.float32),
        grid_spec=pltpu.PrefetchScalarGridSpec(
            num_scalar_prefetch=1,
            grid=(own_modes,),
            in_specs=[
                pl.BlockSpec(memory_space=pltpu.SMEM),
                pl.BlockSpec(memory_space=pltpu.VMEM),
                pl.BlockSpec(memory_space=pltpu.VMEM),
            ],
            out_specs=pl.BlockSpec((1, rows, cols), lambda i, p: (i, 0, 0)),
            scratch_shapes=[pltpu.VMEM((5, kl_terms, rows, cols), jnp.float32)],
        ),
        compiler_params=pltpu.CompilerParams(
            dimension_semantics=("arbitrary",), vmem_limit_bytes=48 * 1024 * 1024
        ),
    )(partners, weights, every, coef)


def rim_kernel(partners, weights, halo, c_rim, applied, out):
    slot = pl.program_id(0)
    kl_terms = c_rim.shape[0]
    rows = out.shape[1]
    cols = out.shape[2]
    fix = jnp.zeros((2, cols), jnp.float32)
    for k in range(kl_terms):
        j0 = partners[slot, 2 * k]
        j1 = partners[slot, 2 * k + 1]
        w0 = weights[slot, 2 * k]
        w1 = weights[slot, 2 * k + 1]
        fix = fix + c_rim[k] * (w0 * halo[j0] + w1 * halo[j1])
    row = lax.broadcasted_iota(jnp.int32, (rows, cols), 0)
    zero = jnp.zeros((rows, cols), jnp.float32)
    spread = jnp.where(row == 0, jnp.broadcast_to(fix[0:1], (rows, cols)), zero)
    spread = jnp.where(row == rows - 1, jnp.broadcast_to(fix[1:2], (rows, cols)), spread)
    out[0] = applied[0] - spread


def rim_apply(applied, halo, c_rim, partners, weights):
    own_modes, rows, cols = applied.shape
    return pl.pallas_call(
        rim_kernel,
        out_shape=jax.ShapeDtypeStruct(applied.shape, jnp.float32),
        grid_spec=pltpu.PrefetchScalarGridSpec(
            num_scalar_prefetch=1,
            grid=(own_modes,),
            in_specs=[
                pl.BlockSpec(memory_space=pltpu.SMEM),
                pl.BlockSpec(memory_space=pltpu.VMEM),
                pl.BlockSpec(memory_space=pltpu.VMEM),
                pl.BlockSpec((1, rows, cols), lambda i, p: (i, 0, 0)),
            ],
            out_specs=pl.BlockSpec((1, rows, cols), lambda i, p: (i, 0, 0)),
        ),
        input_output_aliases={4: 0},
        compiler_params=pltpu.CompilerParams(dimension_semantics=("arbitrary",)),
    )(partners, weights, halo, c_rim, applied)


def solution(mesh):
    return jax.shard_map(
        local,
        mesh=mesh,
        in_specs=(P("chaos", "space", None), P(None, "space", None), P(), P(), P()),
        out_specs=P("chaos", "space", None),
        check_vma=False,
    )
```

```python
import jax
import jax.numpy as jnp
from jax import lax
from jax.experimental import pallas as pl
from jax.experimental.pallas import tpu as pltpu
from jax.sharding import PartitionSpec as P


def extended_2(x, sides, width):
    for axis, dim in sides:
        count, length = (lax.axis_size(axis), x.shape[dim])
        up = [(i, (i + 1) % count) for i in range(count - 1)]
        down = [(j, i) for i, j in up]
        last = lax.slice_in_dim(x, length - width, length, axis=dim)
        first = lax.slice_in_dim(x, 0, width, axis=dim)
        before = lax.ppermute(last, axis, up)
        after = lax.ppermute(first, axis, down)
        x = jnp.concatenate([before, x, after], axis=dim)
    return x


def shift_cols(x, direction):
    zero = jnp.zeros_like(x[..., :1])
    if direction > 0:
        return jnp.concatenate([zero, x[..., :-1]], axis=-1)
    return jnp.concatenate([x[..., 1:], zero], axis=-1)


def coupling_table(triples, ratios, mode_of_slot, kl_terms, mode_count):
    matches = triples[:, :2, None] == mode_of_slot[None, None, :]
    slot_pairs = jnp.sum(jnp.where(matches, jnp.arange(mode_count, dtype=jnp.int32), 0), axis=2)
    weights = ratios[:, 0].astype(jnp.float32) / ratios[:, 1].astype(jnp.float32)
    flat_index = (triples[:, 2] * mode_count + slot_pairs[:, 0]) * mode_count + slot_pairs[:, 1]
    coupling = (
        jnp.zeros((kl_terms * mode_count * mode_count,), jnp.float32).at[flat_index].add(weights)
    )
    return coupling.reshape(kl_terms, mode_count, mode_count)


def neighbour_table(local_rows):
    mode_count = local_rows.shape[-1]
    present = local_rows > 0
    first = jnp.argmax(present, axis=-1).astype(jnp.int32)
    last = (mode_count - 1 - jnp.argmax(present[..., ::-1], axis=-1)).astype(jnp.int32)
    w_first = jnp.take_along_axis(local_rows, first[..., None], axis=-1)[..., 0]
    w_last = jnp.take_along_axis(local_rows, last[..., None], axis=-1)[..., 0]
    w_last = jnp.where(last == first, jnp.zeros_like(w_last), w_last)
    return first, last, w_first, w_last


def shifted(x, step):
    count = lax.axis_size("chaos")
    return lax.ppermute(x, "chaos", [(c, (c + step) % count) for c in range(count)])


def ring_gather(block, tables):
    count = lax.axis_size("chaos")
    me = lax.axis_index("chaos")
    rows = block.shape[1]
    half = block.shape[-1] // 2
    partner = lax.ppermute(block, "chaos", [(c, c ^ 1) for c in range(count)])
    pieces = []
    owners = []
    for base, origin in ((block, me), (partner, me ^ 1)):
        from_left = shifted(base, 2)
        from_right = shifted(base, -2)
        if origin is me:
            from_left, tables = lax.optimization_barrier((from_left, tables))
        far = jnp.concatenate(
            [shifted(from_left[..., :half], 2), shifted(from_right[..., half:], -2)], axis=-1
        )
        pieces += [base, from_left, from_right, far]
        owners += [origin, (origin - 2) % count, (origin + 2) % count, (origin + 4) % count]
    above = []
    below = []
    for piece in pieces:
        a, b = space_halo(piece[:, rows - 1:], piece[:, :1])
        above.append(a)
        below.append(b)
    every = jnp.concatenate(pieces, axis=0)
    halo = jnp.concatenate([jnp.concatenate(above, axis=0), jnp.concatenate(below, axis=0)], axis=1)
    return every, halo, jnp.stack(owners).astype(jnp.int32), tables


def space_halo(edge_last, edge_first):
    count = lax.axis_size("space")
    up = [(i, i + 1) for i in range(count - 1)]
    down = [(i + 1, i) for i in range(count - 1)]
    return lax.ppermute(edge_last, "space", up), lax.ppermute(edge_first, "space", down)


def local(modes, kl_fields, triples, ratios, mode_of_slot):
    groups = lax.axis_size("chaos")
    own_modes = modes.shape[0]
    mode_count = own_modes * groups
    kl_terms = kl_fields.shape[0]
    rows = modes.shape[1]
    count = lax.axis_size("chaos")
    me = lax.axis_index("chaos")
    order = jnp.stack(
        [me, (me - 2) % count, (me + 2) % count, (me + 4) % count,
         me ^ 1, ((me ^ 1) - 2) % count, ((me ^ 1) + 2) % count, ((me ^ 1) + 4) % count]
    ).astype(jnp.int32)

    first_slot = me * own_modes
    coupling = coupling_table(triples, ratios, mode_of_slot, kl_terms, mode_count)
    local_rows = lax.dynamic_slice_in_dim(coupling, first_slot, own_modes, 1)
    first, last, w_first, w_last = neighbour_table(local_rows)
    owner = jnp.arange(mode_count, dtype=jnp.int32) // own_modes
    position = jnp.argmax(order[None, :] == owner[:, None], axis=1).astype(jnp.int32)
    place = position * own_modes + jnp.arange(mode_count, dtype=jnp.int32) % own_modes
    first = place[first]
    last = place[last]
    weights = jnp.stack([w_first, w_last], axis=-1).transpose(1, 0, 2).reshape(own_modes, 2 * kl_terms)
    partners = jnp.stack([first, last], axis=-1).transpose(1, 0, 2).reshape(own_modes, 2 * kl_terms)

    above, below = space_halo(kl_fields[:, rows - 1:], kl_fields[:, :1])
    coef = jnp.concatenate([above, kl_fields, below], axis=1)
    c_rim = 0.5 * jnp.concatenate([coef[:, 1:2] + coef[:, :1], coef[:, rows:rows + 1] + coef[:, rows + 1:]], axis=1)

    every, halo, _, tables = ring_gather(modes, (partners, weights, coef, c_rim))
    partners, weights, coef, c_rim = tables
    return stencil_apply(every, halo, coef, c_rim, partners, weights)


def stencil_kernel(partners, weights, every, halo, coef, c_rim, out, edges):
    slot = pl.program_id(0)
    kl_terms = coef.shape[0]
    rows = out.shape[1]
    cols = out.shape[2]

    @pl.when(slot == 0)
    def _():
        row = lax.broadcasted_iota(jnp.int32, (rows, cols), 0)
        column = lax.broadcasted_iota(jnp.int32, (rows, cols), 1)
        zero = jnp.zeros((rows, cols), jnp.float32)
        for k in range(kl_terms):
            a_c = coef[k, pl.ds(1, rows), :]
            c_up = 0.5 * (a_c + coef[k, pl.ds(0, rows), :])
            c_dn = 0.5 * (a_c + coef[k, pl.ds(2, rows), :])
            c_lf = 0.5 * (a_c + jnp.where(column == 0, zero, pltpu.roll(a_c, 1, 1)))
            c_rt = 0.5 * (a_c + jnp.where(column == cols - 1, zero, pltpu.roll(a_c, cols - 1, 1)))
            edges[0, k] = (c_up + c_dn) + (c_lf + c_rt)
            edges[1, k] = jnp.where(row == 0, zero, c_up)
            edges[2, k] = jnp.where(row == rows - 1, zero, c_dn)
            edges[3, k] = jnp.where(column == 0, zero, c_lf)
            edges[4, k] = jnp.where(column == cols - 1, zero, c_rt)

    acc = jnp.zeros((rows, cols), jnp.float32)
    fix = jnp.zeros((2, cols), jnp.float32)
    for k in range(kl_terms):
        j0 = partners[slot, 2 * k]
        j1 = partners[slot, 2 * k + 1]
        w0 = weights[slot, 2 * k]
        w1 = weights[slot, 2 * k + 1]
        center = w0 * every[j0] + w1 * every[j1]
        up = pltpu.roll(center, 1, 0)
        dn = pltpu.roll(center, rows - 1, 0)
        lf = pltpu.roll(center, 1, 1)
        rt = pltpu.roll(center, cols - 1, 1)
        term = edges[0, k] * center - edges[1, k] * up
        term = term - edges[2, k] * dn
        term = term - edges[3, k] * lf
        term = term - edges[4, k] * rt
        acc = acc + term
        fix = fix + c_rim[k] * (w0 * halo[j0] + w1 * halo[j1])
    row = lax.broadcasted_iota(jnp.int32, (rows, cols), 0)
    spread = jnp.where(row == 0, jnp.broadcast_to(fix[0:1], (rows, cols)), jnp.zeros((rows, cols), jnp.float32))
    spread = jnp.where(row == rows - 1, jnp.broadcast_to(fix[1:2], (rows, cols)), spread)
    out[0] = acc - spread


def stencil_apply(every, halo, coef, c_rim, partners, weights):
    own_modes = partners.shape[0]
    kl_terms = coef.shape[0]
    rows = every.shape[1]
    cols = every.shape[2]
    return pl.pallas_call(
        stencil_kernel,
        out_shape=jax.ShapeDtypeStruct((own_modes, rows, cols), jnp.float32),
        grid_spec=pltpu.PrefetchScalarGridSpec(
            num_scalar_prefetch=1,
            grid=(own_modes,),
            in_specs=[
                pl.BlockSpec(memory_space=pltpu.SMEM),
                pl.BlockSpec(memory_space=pltpu.VMEM),
                pl.BlockSpec(memory_space=pltpu.VMEM),
                pl.BlockSpec(memory_space=pltpu.VMEM),
                pl.BlockSpec(memory_space=pltpu.VMEM),
            ],
            out_specs=pl.BlockSpec((1, rows, cols), lambda i, p: (i, 0, 0)),
            scratch_shapes=[pltpu.VMEM((5, kl_terms, rows, cols), jnp.float32)],
        ),
        compiler_params=pltpu.CompilerParams(
            dimension_semantics=("arbitrary",), vmem_limit_bytes=48 * 1024 * 1024
        ),
    )(partners, weights, every, halo, coef, c_rim)


def solution(mesh):
    return jax.shard_map(
        local,
        mesh=mesh,
        in_specs=(P("chaos", "space", None), P(None, "space", None), P(), P(), P()),
        out_specs=P("chaos", "space", None),
        check_vma=False,
    )
```

```python
import jax
import jax.numpy as jnp
from jax import lax
from jax.experimental import pallas as pl
from jax.experimental.pallas import tpu as pltpu
from jax.sharding import PartitionSpec as P


def extended_2(x, sides, width):
    for axis, dim in sides:
        count, length = (lax.axis_size(axis), x.shape[dim])
        up = [(i, (i + 1) % count) for i in range(count - 1)]
        down = [(j, i) for i, j in up]
        last = lax.slice_in_dim(x, length - width, length, axis=dim)
        first = lax.slice_in_dim(x, 0, width, axis=dim)
        before = lax.ppermute(last, axis, up)
        after = lax.ppermute(first, axis, down)
        x = jnp.concatenate([before, x, after], axis=dim)
    return x


def shift_cols(x, direction):
    zero = jnp.zeros_like(x[..., :1])
    if direction > 0:
        return jnp.concatenate([zero, x[..., :-1]], axis=-1)
    return jnp.concatenate([x[..., 1:], zero], axis=-1)


def coupling_table(triples, ratios, mode_of_slot, kl_terms, mode_count):
    matches = triples[:, :2, None] == mode_of_slot[None, None, :]
    slot_pairs = jnp.sum(jnp.where(matches, jnp.arange(mode_count, dtype=jnp.int32), 0), axis=2)
    weights = ratios[:, 0].astype(jnp.float32) / ratios[:, 1].astype(jnp.float32)
    flat_index = (triples[:, 2] * mode_count + slot_pairs[:, 0]) * mode_count + slot_pairs[:, 1]
    coupling = (
        jnp.zeros((kl_terms * mode_count * mode_count,), jnp.float32).at[flat_index].add(weights)
    )
    return coupling.reshape(kl_terms, mode_count, mode_count)


def neighbour_table(local_rows):
    mode_count = local_rows.shape[-1]
    present = local_rows > 0
    first = jnp.argmax(present, axis=-1).astype(jnp.int32)
    last = (mode_count - 1 - jnp.argmax(present[..., ::-1], axis=-1)).astype(jnp.int32)
    w_first = jnp.take_along_axis(local_rows, first[..., None], axis=-1)[..., 0]
    w_last = jnp.take_along_axis(local_rows, last[..., None], axis=-1)[..., 0]
    w_last = jnp.where(last == first, jnp.zeros_like(w_last), w_last)
    return first, last, w_first, w_last


def shifted(x, step):
    count = lax.axis_size("chaos")
    return lax.ppermute(x, "chaos", [(c, (c + step) % count) for c in range(count)])


def ring_gather(block, tables):
    count = lax.axis_size("chaos")
    me = lax.axis_index("chaos")
    half = block.shape[-1] // 2
    partner = lax.ppermute(block, "chaos", [(c, c ^ 1) for c in range(count)])
    pieces = []
    owners = []
    for base, origin in ((block, me), (partner, me ^ 1)):
        from_left = shifted(base, 2)
        from_right = shifted(base, -2)
        if origin is me:
            from_left, tables = lax.optimization_barrier((from_left, tables))
        far = jnp.concatenate(
            [shifted(from_left[..., :half], 2), shifted(from_right[..., half:], -2)], axis=-1
        )
        pieces += [base, from_left, from_right, far]
        owners += [origin, (origin - 2) % count, (origin + 2) % count, (origin + 4) % count]
    return jnp.concatenate(pieces, axis=0), tables


def space_halo(edge_last, edge_first):
    count = lax.axis_size("space")
    up = [(i, i + 1) for i in range(count - 1)]
    down = [(i + 1, i) for i in range(count - 1)]
    return lax.ppermute(edge_last, "space", up), lax.ppermute(edge_first, "space", down)


def local(modes, kl_fields, triples, ratios, mode_of_slot):
    groups = lax.axis_size("chaos")
    own_modes = modes.shape[0]
    mode_count = own_modes * groups
    kl_terms = kl_fields.shape[0]
    rows = modes.shape[1]
    me = lax.axis_index("chaos")
    order = jnp.stack(
        [me, (me - 2) % groups, (me + 2) % groups, (me + 4) % groups,
         me ^ 1, ((me ^ 1) - 2) % groups, ((me ^ 1) + 2) % groups, ((me ^ 1) + 4) % groups]
    ).astype(jnp.int32)

    first_slot = me * own_modes
    coupling = coupling_table(triples, ratios, mode_of_slot, kl_terms, mode_count)
    local_rows = lax.dynamic_slice_in_dim(coupling, first_slot, own_modes, 1)
    first, last, w_first, w_last = neighbour_table(local_rows)
    owner = jnp.arange(mode_count, dtype=jnp.int32) // own_modes
    position = jnp.argmax(order[None, :] == owner[:, None], axis=1).astype(jnp.int32)
    place = position * own_modes + jnp.arange(mode_count, dtype=jnp.int32) % own_modes
    first = place[first]
    last = place[last]
    weights = jnp.stack([w_first, w_last], axis=-1).transpose(1, 0, 2).reshape(own_modes, 2 * kl_terms)
    partners = jnp.stack([first, last], axis=-1).transpose(1, 0, 2).reshape(own_modes, 2 * kl_terms)

    above, below = space_halo(kl_fields[:, rows - 1:], kl_fields[:, :1])
    coef = jnp.concatenate([above, kl_fields, below], axis=1)

    every, tables = ring_gather(modes, (partners, weights, coef))
    partners, weights, coef = tables
    applied, to_prev, to_next = stencil_apply(every, coef, partners, weights)

    from_prev, from_next = space_halo(to_next, to_prev)
    top = applied[:, :1] - from_prev[:, None]
    bottom = applied[:, rows - 1:] - from_next[:, None]
    applied = lax.dynamic_update_slice_in_dim(applied, top, 0, 1)
    applied = lax.dynamic_update_slice_in_dim(applied, bottom, rows - 1, 1)
    return applied


def stencil_kernel(partners, weights, every, coef, out, to_prev, to_next, edges):
    slot = pl.program_id(0)
    kl_terms = coef.shape[0]
    rows = out.shape[1]
    cols = out.shape[2]

    @pl.when(slot == 0)
    def _():
        row = lax.broadcasted_iota(jnp.int32, (rows, cols), 0)
        column = lax.broadcasted_iota(jnp.int32, (rows, cols), 1)
        zero = jnp.zeros((rows, cols), jnp.float32)
        for k in range(kl_terms):
            a_c = coef[k, pl.ds(1, rows), :]
            c_up = 0.5 * (a_c + coef[k, pl.ds(0, rows), :])
            c_dn = 0.5 * (a_c + coef[k, pl.ds(2, rows), :])
            c_lf = 0.5 * (a_c + jnp.where(column == 0, zero, pltpu.roll(a_c, 1, 1)))
            c_rt = 0.5 * (a_c + jnp.where(column == cols - 1, zero, pltpu.roll(a_c, cols - 1, 1)))
            edges[0, k] = (c_up + c_dn) + (c_lf + c_rt)
            edges[1, k] = jnp.where(row == 0, zero, c_up)
            edges[2, k] = jnp.where(row == rows - 1, zero, c_dn)
            edges[3, k] = jnp.where(column == 0, zero, c_lf)
            edges[4, k] = jnp.where(column == cols - 1, zero, c_rt)
            edges[5, k] = jnp.where(row == 0, c_up, jnp.where(row == rows - 1, c_dn, zero))

    acc = jnp.zeros((rows, cols), jnp.float32)
    rim = jnp.zeros((rows, cols), jnp.float32)
    for k in range(kl_terms):
        j0 = partners[slot, 2 * k]
        j1 = partners[slot, 2 * k + 1]
        w0 = weights[slot, 2 * k]
        w1 = weights[slot, 2 * k + 1]
        center = w0 * every[j0] + w1 * every[j1]
        up = pltpu.roll(center, 1, 0)
        dn = pltpu.roll(center, rows - 1, 0)
        lf = pltpu.roll(center, 1, 1)
        rt = pltpu.roll(center, cols - 1, 1)
        term = edges[0, k] * center - edges[1, k] * up
        term = term - edges[2, k] * dn
        term = term - edges[3, k] * lf
        term = term - edges[4, k] * rt
        acc = acc + term
        rim = rim + edges[5, k] * center
    out[0] = acc
    to_prev[pl.ds(slot, 1), :] = rim[0:1]
    to_next[pl.ds(slot, 1), :] = rim[rows - 1:rows]


def stencil_apply(every, coef, partners, weights):
    own_modes = partners.shape[0]
    kl_terms = coef.shape[0]
    rows = every.shape[1]
    cols = every.shape[2]
    return pl.pallas_call(
        stencil_kernel,
        out_shape=(
            jax.ShapeDtypeStruct((own_modes, rows, cols), jnp.float32),
            jax.ShapeDtypeStruct((own_modes, cols), jnp.float32),
            jax.ShapeDtypeStruct((own_modes, cols), jnp.float32),
        ),
        grid_spec=pltpu.PrefetchScalarGridSpec(
            num_scalar_prefetch=1,
            grid=(own_modes,),
            in_specs=[
                pl.BlockSpec(memory_space=pltpu.SMEM),
                pl.BlockSpec(memory_space=pltpu.VMEM),
                pl.BlockSpec(memory_space=pltpu.VMEM),
            ],
            out_specs=(
                pl.BlockSpec((1, rows, cols), lambda i, p: (i, 0, 0)),
                pl.BlockSpec(memory_space=pltpu.VMEM),
                pl.BlockSpec(memory_space=pltpu.VMEM),
            ),
            scratch_shapes=[pltpu.VMEM((6, kl_terms, rows, cols), jnp.float32)],
        ),
        compiler_params=pltpu.CompilerParams(
            dimension_semantics=("arbitrary",), vmem_limit_bytes=48 * 1024 * 1024
        ),
    )(partners, weights, every, coef)


def solution(mesh):
    return jax.shard_map(
        local,
        mesh=mesh,
        in_specs=(P("chaos", "space", None), P(None, "space", None), P(), P(), P()),
        out_specs=P("chaos", "space", None),
        check_vma=False,
    )
```

```python
import jax
import jax.numpy as jnp
from jax import lax
from jax.experimental import pallas as pl
from jax.experimental.pallas import tpu as pltpu
from jax.sharding import PartitionSpec as P


def extended_2(x, sides, width):
    for axis, dim in sides:
        count, length = (lax.axis_size(axis), x.shape[dim])
        up = [(i, (i + 1) % count) for i in range(count - 1)]
        down = [(j, i) for i, j in up]
        last = lax.slice_in_dim(x, length - width, length, axis=dim)
        first = lax.slice_in_dim(x, 0, width, axis=dim)
        before = lax.ppermute(last, axis, up)
        after = lax.ppermute(first, axis, down)
        x = jnp.concatenate([before, x, after], axis=dim)
    return x


def shift_cols(x, direction):
    zero = jnp.zeros_like(x[..., :1])
    if direction > 0:
        return jnp.concatenate([zero, x[..., :-1]], axis=-1)
    return jnp.concatenate([x[..., 1:], zero], axis=-1)


def coupling_table(triples, ratios, mode_of_slot, kl_terms, mode_count):
    matches = triples[:, :2, None] == mode_of_slot[None, None, :]
    slot_pairs = jnp.sum(jnp.where(matches, jnp.arange(mode_count, dtype=jnp.int32), 0), axis=2)
    weights = ratios[:, 0].astype(jnp.float32) / ratios[:, 1].astype(jnp.float32)
    flat_index = (triples[:, 2] * mode_count + slot_pairs[:, 0]) * mode_count + slot_pairs[:, 1]
    coupling = (
        jnp.zeros((kl_terms * mode_count * mode_count,), jnp.float32).at[flat_index].add(weights)
    )
    return coupling.reshape(kl_terms, mode_count, mode_count)


def neighbour_table(local_rows):
    mode_count = local_rows.shape[-1]
    present = local_rows > 0
    first = jnp.argmax(present, axis=-1).astype(jnp.int32)
    last = (mode_count - 1 - jnp.argmax(present[..., ::-1], axis=-1)).astype(jnp.int32)
    w_first = jnp.take_along_axis(local_rows, first[..., None], axis=-1)[..., 0]
    w_last = jnp.take_along_axis(local_rows, last[..., None], axis=-1)[..., 0]
    w_last = jnp.where(last == first, jnp.zeros_like(w_last), w_last)
    return first, last, w_first, w_last


def shifted(x, step):
    count = lax.axis_size("chaos")
    return lax.ppermute(x, "chaos", [(c, (c + step) % count) for c in range(count)])


def ring_gather(block, tables):
    count = lax.axis_size("chaos")
    me = lax.axis_index("chaos")
    half = block.shape[-1] // 2
    partner = lax.ppermute(block, "chaos", [(c, c ^ 1) for c in range(count)])
    pieces = []
    owners = []
    for base, origin in ((block, me), (partner, me ^ 1)):
        from_left = shifted(base, 2)
        from_right = shifted(base, -2)
        if origin is not me:
            from_left, tables = lax.optimization_barrier((from_left, tables))
        far = jnp.concatenate(
            [shifted(from_left[..., :half], 2), shifted(from_right[..., half:], -2)], axis=-1
        )
        pieces += [base, from_left, from_right, far]
        owners += [origin, (origin - 2) % count, (origin + 2) % count, (origin + 4) % count]
    return jnp.concatenate(pieces, axis=0), tables


def space_halo(edge_last, edge_first):
    count = lax.axis_size("space")
    up = [(i, i + 1) for i in range(count - 1)]
    down = [(i + 1, i) for i in range(count - 1)]
    return lax.ppermute(edge_last, "space", up), lax.ppermute(edge_first, "space", down)


def local(modes, kl_fields, triples, ratios, mode_of_slot):
    groups = lax.axis_size("chaos")
    own_modes = modes.shape[0]
    mode_count = own_modes * groups
    kl_terms = kl_fields.shape[0]
    rows = modes.shape[1]
    me = lax.axis_index("chaos")
    order = jnp.stack(
        [me, (me - 2) % groups, (me + 2) % groups, (me + 4) % groups,
         me ^ 1, ((me ^ 1) - 2) % groups, ((me ^ 1) + 2) % groups, ((me ^ 1) + 4) % groups]
    ).astype(jnp.int32)

    first_slot = me * own_modes
    coupling = coupling_table(triples, ratios, mode_of_slot, kl_terms, mode_count)
    local_rows = lax.dynamic_slice_in_dim(coupling, first_slot, own_modes, 1)
    first, last, w_first, w_last = neighbour_table(local_rows)
    owner = jnp.arange(mode_count, dtype=jnp.int32) // own_modes
    position = jnp.argmax(order[None, :] == owner[:, None], axis=1).astype(jnp.int32)
    place = position * own_modes + jnp.arange(mode_count, dtype=jnp.int32) % own_modes
    first = place[first]
    last = place[last]
    weights = jnp.stack([w_first, w_last], axis=-1).transpose(1, 0, 2).reshape(own_modes, 2 * kl_terms)
    partners = jnp.stack([first, last], axis=-1).transpose(1, 0, 2).reshape(own_modes, 2 * kl_terms)

    above, below = space_halo(kl_fields[:, rows - 1:], kl_fields[:, :1])
    coef = jnp.concatenate([above, kl_fields, below], axis=1)

    every, tables = ring_gather(modes, (partners, weights, coef))
    partners, weights, coef = tables
    applied, to_prev, to_next = stencil_apply(every, coef, partners, weights)

    from_prev, from_next = space_halo(to_next, to_prev)
    row = lax.broadcasted_iota(jnp.int32, applied.shape, 1)
    rim = jnp.where(row == 0, from_prev[:, None], jnp.where(row == rows - 1, from_next[:, None], 0.0))
    return applied - rim


def stencil_kernel(partners, weights, every, coef, out, to_prev, to_next, edges):
    slot = pl.program_id(0)
    kl_terms = coef.shape[0]
    rows = out.shape[1]
    cols = out.shape[2]

    @pl.when(slot == 0)
    def _():
        row = lax.broadcasted_iota(jnp.int32, (rows, cols), 0)
        column = lax.broadcasted_iota(jnp.int32, (rows, cols), 1)
        zero = jnp.zeros((rows, cols), jnp.float32)
        for k in range(kl_terms):
            a_c = coef[k, pl.ds(1, rows), :]
            c_up = 0.5 * (a_c + coef[k, pl.ds(0, rows), :])
            c_dn = 0.5 * (a_c + coef[k, pl.ds(2, rows), :])
            c_lf = 0.5 * (a_c + jnp.where(column == 0, zero, pltpu.roll(a_c, 1, 1)))
            c_rt = 0.5 * (a_c + jnp.where(column == cols - 1, zero, pltpu.roll(a_c, cols - 1, 1)))
            edges[0, k] = (c_up + c_dn) + (c_lf + c_rt)
            edges[1, k] = jnp.where(row == 0, zero, c_up)
            edges[2, k] = jnp.where(row == rows - 1, zero, c_dn)
            edges[3, k] = jnp.where(column == 0, zero, c_lf)
            edges[4, k] = jnp.where(column == cols - 1, zero, c_rt)
            edges[5, k] = jnp.where(row == 0, c_up, jnp.where(row == rows - 1, c_dn, zero))

    acc = jnp.zeros((rows, cols), jnp.float32)
    rim = jnp.zeros((rows, cols), jnp.float32)
    for k in range(kl_terms):
        j0 = partners[slot, 2 * k]
        j1 = partners[slot, 2 * k + 1]
        w0 = weights[slot, 2 * k]
        w1 = weights[slot, 2 * k + 1]
        center = w0 * every[j0] + w1 * every[j1]
        up = pltpu.roll(center, 1, 0)
        dn = pltpu.roll(center, rows - 1, 0)
        lf = pltpu.roll(center, 1, 1)
        rt = pltpu.roll(center, cols - 1, 1)
        term = edges[0, k] * center - edges[1, k] * up
        term = term - edges[2, k] * dn
        term = term - edges[3, k] * lf
        term = term - edges[4, k] * rt
        acc = acc + term
        rim = rim + edges[5, k] * center
    out[0] = acc
    to_prev[pl.ds(slot, 1), :] = rim[0:1]
    to_next[pl.ds(slot, 1), :] = rim[rows - 1:rows]


def stencil_apply(every, coef, partners, weights):
    own_modes = partners.shape[0]
    kl_terms = coef.shape[0]
    rows = every.shape[1]
    cols = every.shape[2]
    return pl.pallas_call(
        stencil_kernel,
        out_shape=(
            jax.ShapeDtypeStruct((own_modes, rows, cols), jnp.float32),
            jax.ShapeDtypeStruct((own_modes, cols), jnp.float32),
            jax.ShapeDtypeStruct((own_modes, cols), jnp.float32),
        ),
        grid_spec=pltpu.PrefetchScalarGridSpec(
            num_scalar_prefetch=1,
            grid=(own_modes,),
            in_specs=[
                pl.BlockSpec(memory_space=pltpu.SMEM),
                pl.BlockSpec(memory_space=pltpu.VMEM),
                pl.BlockSpec(memory_space=pltpu.VMEM),
            ],
            out_specs=(
                pl.BlockSpec((1, rows, cols), lambda i, p: (i, 0, 0)),
                pl.BlockSpec(memory_space=pltpu.VMEM),
                pl.BlockSpec(memory_space=pltpu.VMEM),
            ),
            scratch_shapes=[pltpu.VMEM((6, kl_terms, rows, cols), jnp.float32)],
        ),
        compiler_params=pltpu.CompilerParams(
            dimension_semantics=("arbitrary",), vmem_limit_bytes=48 * 1024 * 1024
        ),
    )(partners, weights, every, coef)


def solution(mesh):
    return jax.shard_map(
        local,
        mesh=mesh,
        in_specs=(P("chaos", "space", None), P(None, "space", None), P(), P(), P()),
        out_specs=P("chaos", "space", None),
        check_vma=False,
    )
```

```python
import jax
import jax.numpy as jnp
from jax import lax
from jax.experimental import pallas as pl
from jax.experimental.pallas import tpu as pltpu
from jax.sharding import PartitionSpec as P


def extended_2(x, sides, width):
    for axis, dim in sides:
        count, length = (lax.axis_size(axis), x.shape[dim])
        up = [(i, (i + 1) % count) for i in range(count - 1)]
        down = [(j, i) for i, j in up]
        last = lax.slice_in_dim(x, length - width, length, axis=dim)
        first = lax.slice_in_dim(x, 0, width, axis=dim)
        before = lax.ppermute(last, axis, up)
        after = lax.ppermute(first, axis, down)
        x = jnp.concatenate([before, x, after], axis=dim)
    return x


def shift_cols(x, direction):
    zero = jnp.zeros_like(x[..., :1])
    if direction > 0:
        return jnp.concatenate([zero, x[..., :-1]], axis=-1)
    return jnp.concatenate([x[..., 1:], zero], axis=-1)


def coupling_table(triples, ratios, mode_of_slot, kl_terms, mode_count):
    matches = triples[:, :2, None] == mode_of_slot[None, None, :]
    slot_pairs = jnp.sum(jnp.where(matches, jnp.arange(mode_count, dtype=jnp.int32), 0), axis=2)
    weights = ratios[:, 0].astype(jnp.float32) / ratios[:, 1].astype(jnp.float32)
    flat_index = (triples[:, 2] * mode_count + slot_pairs[:, 0]) * mode_count + slot_pairs[:, 1]
    coupling = (
        jnp.zeros((kl_terms * mode_count * mode_count,), jnp.float32).at[flat_index].add(weights)
    )
    return coupling.reshape(kl_terms, mode_count, mode_count)


def neighbour_table(local_rows):
    mode_count = local_rows.shape[-1]
    present = local_rows > 0
    first = jnp.argmax(present, axis=-1).astype(jnp.int32)
    last = (mode_count - 1 - jnp.argmax(present[..., ::-1], axis=-1)).astype(jnp.int32)
    w_first = jnp.take_along_axis(local_rows, first[..., None], axis=-1)[..., 0]
    w_last = jnp.take_along_axis(local_rows, last[..., None], axis=-1)[..., 0]
    w_last = jnp.where(last == first, jnp.zeros_like(w_last), w_last)
    return first, last, w_first, w_last


def shifted(x, step):
    count = lax.axis_size("chaos")
    return lax.ppermute(x, "chaos", [(c, (c + step) % count) for c in range(count)])


def ring_gather(block, tables):
    count = lax.axis_size("chaos")
    me = lax.axis_index("chaos")
    half = block.shape[-1] // 2
    own_left = shifted(block, 2)
    own_right = shifted(block, -2)
    partner = lax.ppermute(block, "chaos", [(c, c ^ 1) for c in range(count)])
    pieces = []
    owners = []
    for base, origin in ((block, me), (partner, me ^ 1)):
        if origin is me:
            from_left, from_right = own_left, own_right
        else:
            from_left = shifted(base, 2)
            from_right = shifted(base, -2)
        if origin is not me:
            from_left, tables = lax.optimization_barrier((from_left, tables))
        far = jnp.concatenate(
            [shifted(from_left[..., :half], 2), shifted(from_right[..., half:], -2)], axis=-1
        )
        pieces += [base, from_left, from_right, far]
        owners += [origin, (origin - 2) % count, (origin + 2) % count, (origin + 4) % count]
    return jnp.concatenate(pieces, axis=0), tables


def space_halo(edge_last, edge_first):
    count = lax.axis_size("space")
    up = [(i, i + 1) for i in range(count - 1)]
    down = [(i + 1, i) for i in range(count - 1)]
    return lax.ppermute(edge_last, "space", up), lax.ppermute(edge_first, "space", down)


def local(modes, kl_fields, triples, ratios, mode_of_slot):
    groups = lax.axis_size("chaos")
    own_modes = modes.shape[0]
    mode_count = own_modes * groups
    kl_terms = kl_fields.shape[0]
    rows = modes.shape[1]
    me = lax.axis_index("chaos")
    order = jnp.stack(
        [me, (me - 2) % groups, (me + 2) % groups, (me + 4) % groups,
         me ^ 1, ((me ^ 1) - 2) % groups, ((me ^ 1) + 2) % groups, ((me ^ 1) + 4) % groups]
    ).astype(jnp.int32)

    first_slot = me * own_modes
    coupling = coupling_table(triples, ratios, mode_of_slot, kl_terms, mode_count)
    local_rows = lax.dynamic_slice_in_dim(coupling, first_slot, own_modes, 1)
    first, last, w_first, w_last = neighbour_table(local_rows)
    owner = jnp.arange(mode_count, dtype=jnp.int32) // own_modes
    position = jnp.argmax(order[None, :] == owner[:, None], axis=1).astype(jnp.int32)
    place = position * own_modes + jnp.arange(mode_count, dtype=jnp.int32) % own_modes
    first = place[first]
    last = place[last]
    weights = jnp.stack([w_first, w_last], axis=-1).transpose(1, 0, 2).reshape(own_modes, 2 * kl_terms)
    partners = jnp.stack([first, last], axis=-1).transpose(1, 0, 2).reshape(own_modes, 2 * kl_terms)

    above, below = space_halo(kl_fields[:, rows - 1:], kl_fields[:, :1])
    coef = jnp.concatenate([above, kl_fields, below], axis=1)

    every, tables = ring_gather(modes, (partners, weights, coef))
    partners, weights, coef = tables
    to_prev, to_next = rim_apply(every, coef, partners, weights)
    applied = stencil_apply(every, coef, partners, weights)

    from_prev, from_next = space_halo(to_next, to_prev)
    row = lax.broadcasted_iota(jnp.int32, applied.shape, 1)
    rim = jnp.where(row == 0, from_prev[:, None], jnp.where(row == rows - 1, from_next[:, None], 0.0))
    return applied - rim


def stencil_kernel(partners, weights, every, coef, out, edges):
    slot = pl.program_id(0)
    kl_terms = coef.shape[0]
    rows = out.shape[1]
    cols = out.shape[2]

    @pl.when(slot == 0)
    def _():
        row = lax.broadcasted_iota(jnp.int32, (rows, cols), 0)
        column = lax.broadcasted_iota(jnp.int32, (rows, cols), 1)
        zero = jnp.zeros((rows, cols), jnp.float32)
        for k in range(kl_terms):
            a_c = coef[k, pl.ds(1, rows), :]
            c_up = 0.5 * (a_c + coef[k, pl.ds(0, rows), :])
            c_dn = 0.5 * (a_c + coef[k, pl.ds(2, rows), :])
            c_lf = 0.5 * (a_c + jnp.where(column == 0, zero, pltpu.roll(a_c, 1, 1)))
            c_rt = 0.5 * (a_c + jnp.where(column == cols - 1, zero, pltpu.roll(a_c, cols - 1, 1)))
            edges[0, k] = (c_up + c_dn) + (c_lf + c_rt)
            edges[1, k] = jnp.where(row == 0, zero, c_up)
            edges[2, k] = jnp.where(row == rows - 1, zero, c_dn)
            edges[3, k] = jnp.where(column == 0, zero, c_lf)
            edges[4, k] = jnp.where(column == cols - 1, zero, c_rt)

    acc = jnp.zeros((rows, cols), jnp.float32)
    for k in range(kl_terms):
        j0 = partners[slot, 2 * k]
        j1 = partners[slot, 2 * k + 1]
        w0 = weights[slot, 2 * k]
        w1 = weights[slot, 2 * k + 1]
        center = w0 * every[j0] + w1 * every[j1]
        up = pltpu.roll(center, 1, 0)
        dn = pltpu.roll(center, rows - 1, 0)
        lf = pltpu.roll(center, 1, 1)
        rt = pltpu.roll(center, cols - 1, 1)
        term = edges[0, k] * center - edges[1, k] * up
        term = term - edges[2, k] * dn
        term = term - edges[3, k] * lf
        term = term - edges[4, k] * rt
        acc = acc + term
    out[0] = acc


def stencil_apply(every, coef, partners, weights):
    own_modes = partners.shape[0]
    kl_terms = coef.shape[0]
    rows = every.shape[1]
    cols = every.shape[2]
    return pl.pallas_call(
        stencil_kernel,
        out_shape=jax.ShapeDtypeStruct((own_modes, rows, cols), jnp.float32),
        grid_spec=pltpu.PrefetchScalarGridSpec(
            num_scalar_prefetch=1,
            grid=(own_modes,),
            in_specs=[
                pl.BlockSpec(memory_space=pltpu.SMEM),
                pl.BlockSpec(memory_space=pltpu.VMEM),
                pl.BlockSpec(memory_space=pltpu.VMEM),
            ],
            out_specs=pl.BlockSpec((1, rows, cols), lambda i, p: (i, 0, 0)),
            scratch_shapes=[pltpu.VMEM((5, kl_terms, rows, cols), jnp.float32)],
        ),
        compiler_params=pltpu.CompilerParams(
            dimension_semantics=("arbitrary",), vmem_limit_bytes=48 * 1024 * 1024
        ),
    )(partners, weights, every, coef)


def rim_kernel(partners, weights, every, coef, to_prev, to_next):
    own_modes, cols = to_prev.shape
    kl_terms = coef.shape[0]
    rows = every.shape[1]

    def one_slot(slot, carry):
        first = jnp.zeros((1, cols), jnp.float32)
        last = jnp.zeros((1, cols), jnp.float32)
        for k in range(kl_terms):
            j0 = partners[slot, 2 * k]
            j1 = partners[slot, 2 * k + 1]
            w0 = weights[slot, 2 * k]
            w1 = weights[slot, 2 * k + 1]
            c_first = 0.5 * (coef[k, pl.ds(1, 1), :] + coef[k, pl.ds(0, 1), :])
            c_last = 0.5 * (coef[k, pl.ds(rows, 1), :] + coef[k, pl.ds(rows + 1, 1), :])
            first = first + c_first * (w0 * every[j0, pl.ds(0, 1), :] + w1 * every[j1, pl.ds(0, 1), :])
            last = last + c_last * (w0 * every[j0, pl.ds(rows - 1, 1), :] + w1 * every[j1, pl.ds(rows - 1, 1), :])
        to_prev[pl.ds(slot, 1), :] = first
        to_next[pl.ds(slot, 1), :] = last
        return carry

    lax.fori_loop(0, own_modes, one_slot, 0)


def rim_apply(every, coef, partners, weights):
    own_modes = partners.shape[0]
    cols = every.shape[2]
    return pl.pallas_call(
        rim_kernel,
        out_shape=(
            jax.ShapeDtypeStruct((own_modes, cols), jnp.float32),
            jax.ShapeDtypeStruct((own_modes, cols), jnp.float32),
        ),
        grid_spec=pltpu.PrefetchScalarGridSpec(
            num_scalar_prefetch=1,
            grid=(),
            in_specs=[pl.BlockSpec(memory_space=pltpu.SMEM)] + [pl.BlockSpec(memory_space=pltpu.VMEM)] * 2,
            out_specs=(pl.BlockSpec(memory_space=pltpu.VMEM), pl.BlockSpec(memory_space=pltpu.VMEM)),
        ),
        compiler_params=pltpu.CompilerParams(vmem_limit_bytes=48 * 1024 * 1024),
    )(partners, weights, every, coef)


def solution(mesh):
    return jax.shard_map(
        local,
        mesh=mesh,
        in_specs=(P("chaos", "space", None), P(None, "space", None), P(), P(), P()),
        out_specs=P("chaos", "space", None),
        check_vma=False,
    )
```

```python
import jax
import jax.numpy as jnp
from jax import lax
from jax.experimental import pallas as pl
from jax.experimental.pallas import tpu as pltpu
from jax.sharding import PartitionSpec as P


def shift_cols(x, direction):
    zero = jnp.zeros_like(x[..., :1])
    if direction > 0:
        return jnp.concatenate([zero, x[..., :-1]], axis=-1)
    return jnp.concatenate([x[..., 1:], zero], axis=-1)


def shifted(x, step):
    count = lax.axis_size("chaos")
    return lax.ppermute(x, "chaos", [(c, (c + step) % count) for c in range(count)])


def ring_gather(block, tables):
    count = lax.axis_size("chaos")
    me = lax.axis_index("chaos")
    half = block.shape[-1] // 2
    partner = lax.ppermute(block, "chaos", [(c, c ^ 1) for c in range(count)])
    pieces = []
    owners = []
    for base, origin in ((block, me), (partner, me ^ 1)):
        from_left = shifted(base, 2)
        from_right = shifted(base, -2)
        if origin is not me:
            from_left, tables = lax.optimization_barrier((from_left, tables))
        far = jnp.concatenate(
            [shifted(from_left[..., :half], 2), shifted(from_right[..., half:], -2)], axis=-1
        )
        pieces += [base, from_left, from_right, far]
        owners += [origin, (origin - 2) % count, (origin + 2) % count, (origin + 4) % count]
    return jnp.concatenate(pieces, axis=0), tables


def space_halo(edge_last, edge_first):
    count = lax.axis_size("space")
    up = [(i, i + 1) for i in range(count - 1)]
    down = [(i + 1, i) for i in range(count - 1)]
    return lax.ppermute(edge_last, "space", up), lax.ppermute(edge_first, "space", down)


def local(modes, kl_fields, triples, ratios, mode_of_slot):
    groups = lax.axis_size("chaos")
    own_modes = modes.shape[0]
    mode_count = own_modes * groups
    kl_terms = kl_fields.shape[0]
    rows = modes.shape[1]
    me = lax.axis_index("chaos")
    order = jnp.stack(
        [me, (me - 2) % groups, (me + 2) % groups, (me + 4) % groups,
         me ^ 1, ((me ^ 1) - 2) % groups, ((me ^ 1) + 2) % groups, ((me ^ 1) + 4) % groups]
    ).astype(jnp.int32)

    slot_ids = jnp.arange(mode_count, dtype=jnp.int32)
    slot_of_mode = jnp.sum(jnp.where(mode_of_slot[None, :] == slot_ids[:, None], slot_ids[None, :], 0), axis=1)
    position = jnp.argmax(order[None, :] == (slot_ids // own_modes)[:, None], axis=1).astype(jnp.int32)
    place = position * own_modes + slot_ids % own_modes
    local_modes = lax.dynamic_slice_in_dim(mode_of_slot, me * own_modes, own_modes)
    row_count = triples.shape[0]
    hit = (triples[None, None, :, 0] == local_modes[:, None, None]) & (
        triples[None, None, :, 2] == jnp.arange(kl_terms, dtype=jnp.int32)[None, :, None]
    )
    found = jnp.any(hit, axis=-1)
    t0 = jnp.argmax(hit, axis=-1).astype(jnp.int32)
    t1 = (row_count - 1 - jnp.argmax(hit[..., ::-1], axis=-1)).astype(jnp.int32)
    row_weight = ratios[:, 0].astype(jnp.float32) / ratios[:, 1].astype(jnp.float32)
    w_first = jnp.where(found, row_weight[t0], 0.0)
    w_last = jnp.where(found & (t1 != t0), row_weight[t1], 0.0)
    first = place[slot_of_mode[triples[t0, 1]]]
    last = place[slot_of_mode[triples[t1, 1]]]
    weights = jnp.stack([w_first, w_last], axis=-1).reshape(own_modes, 2 * kl_terms)
    partners = jnp.stack([first, last], axis=-1).reshape(own_modes, 2 * kl_terms)

    above, below = space_halo(kl_fields[:, rows - 1:], kl_fields[:, :1])
    coef = jnp.concatenate([above, kl_fields, below], axis=1)

    every, tables = ring_gather(modes, (partners, weights, coef))
    partners, weights, coef = tables
    applied, to_prev, to_next = stencil_apply(every, coef, partners, weights)

    from_prev, from_next = space_halo(to_next, to_prev)
    row = lax.broadcasted_iota(jnp.int32, applied.shape, 1)
    rim = jnp.where(row == 0, from_prev[:, None], jnp.where(row == rows - 1, from_next[:, None], 0.0))
    return applied - rim


def stencil_kernel(partners, weights, every, coef, out, to_prev, to_next, edges):
    slot = pl.program_id(0)
    kl_terms = coef.shape[0]
    rows = out.shape[1]
    cols = out.shape[2]

    @pl.when(slot == 0)
    def _():
        row = lax.broadcasted_iota(jnp.int32, (rows, cols), 0)
        column = lax.broadcasted_iota(jnp.int32, (rows, cols), 1)
        zero = jnp.zeros((rows, cols), jnp.float32)
        for k in range(kl_terms):
            a_c = coef[k, pl.ds(1, rows), :]
            c_up = 0.5 * (a_c + coef[k, pl.ds(0, rows), :])
            c_dn = 0.5 * (a_c + coef[k, pl.ds(2, rows), :])
            c_lf = 0.5 * (a_c + jnp.where(column == 0, zero, pltpu.roll(a_c, 1, 1)))
            c_rt = 0.5 * (a_c + jnp.where(column == cols - 1, zero, pltpu.roll(a_c, cols - 1, 1)))
            edges[0, k] = (c_up + c_dn) + (c_lf + c_rt)
            edges[1, k] = jnp.where(row == 0, zero, c_up)
            edges[2, k] = jnp.where(row == rows - 1, zero, c_dn)
            edges[3, k] = jnp.where(column == 0, zero, c_lf)
            edges[4, k] = jnp.where(column == cols - 1, zero, c_rt)
            edges[5, k] = jnp.where(row == 0, c_up, jnp.where(row == rows - 1, c_dn, zero))

    acc = jnp.zeros((rows, cols), jnp.float32)
    rim = jnp.zeros((rows, cols), jnp.float32)
    for k in range(kl_terms):
        j0 = partners[slot, 2 * k]
        j1 = partners[slot, 2 * k + 1]
        w0 = weights[slot, 2 * k]
        w1 = weights[slot, 2 * k + 1]
        center = w0 * every[j0] + w1 * every[j1]
        up = pltpu.roll(center, 1, 0)
        dn = pltpu.roll(center, rows - 1, 0)
        lf = pltpu.roll(center, 1, 1)
        rt = pltpu.roll(center, cols - 1, 1)
        term = edges[0, k] * center - edges[1, k] * up
        term = term - edges[2, k] * dn
        term = term - edges[3, k] * lf
        term = term - edges[4, k] * rt
        acc = acc + term
        rim = rim + edges[5, k] * center
    out[0] = acc
    to_prev[pl.ds(slot, 1), :] = rim[0:1]
    to_next[pl.ds(slot, 1), :] = rim[rows - 1:rows]


def stencil_apply(every, coef, partners, weights):
    own_modes = partners.shape[0]
    kl_terms = coef.shape[0]
    rows = every.shape[1]
    cols = every.shape[2]
    return pl.pallas_call(
        stencil_kernel,
        out_shape=(
            jax.ShapeDtypeStruct((own_modes, rows, cols), jnp.float32),
            jax.ShapeDtypeStruct((own_modes, cols), jnp.float32),
            jax.ShapeDtypeStruct((own_modes, cols), jnp.float32),
        ),
        grid_spec=pltpu.PrefetchScalarGridSpec(
            num_scalar_prefetch=1,
            grid=(own_modes,),
            in_specs=[
                pl.BlockSpec(memory_space=pltpu.SMEM),
                pl.BlockSpec(memory_space=pltpu.VMEM),
                pl.BlockSpec(memory_space=pltpu.VMEM),
            ],
            out_specs=(
                pl.BlockSpec((1, rows, cols), lambda i, p: (i, 0, 0)),
                pl.BlockSpec(memory_space=pltpu.VMEM),
                pl.BlockSpec(memory_space=pltpu.VMEM),
            ),
            scratch_shapes=[pltpu.VMEM((6, kl_terms, rows, cols), jnp.float32)],
        ),
        compiler_params=pltpu.CompilerParams(
            dimension_semantics=("arbitrary",), vmem_limit_bytes=48 * 1024 * 1024
        ),
    )(partners, weights, every, coef)


def solution(mesh):
    return jax.shard_map(
        local,
        mesh=mesh,
        in_specs=(P("chaos", "space", None), P(None, "space", None), P(), P(), P()),
        out_specs=P("chaos", "space", None),
        check_vma=False,
    )
```

```python
import jax
import jax.numpy as jnp
from jax import lax
from jax.experimental import pallas as pl
from jax.experimental.pallas import tpu as pltpu
from jax.sharding import PartitionSpec as P


def shift_cols(x, direction):
    zero = jnp.zeros_like(x[..., :1])
    if direction > 0:
        return jnp.concatenate([zero, x[..., :-1]], axis=-1)
    return jnp.concatenate([x[..., 1:], zero], axis=-1)


def shifted(x, step):
    count = lax.axis_size("chaos")
    return lax.ppermute(x, "chaos", [(c, (c + step) % count) for c in range(count)])


def ring_gather(block, tables):
    count = lax.axis_size("chaos")
    me = lax.axis_index("chaos")
    half = block.shape[-1] // 2
    partner = lax.ppermute(block, "chaos", [(c, c ^ 1) for c in range(count)])
    pieces = []
    owners = []
    for base, origin in ((block, me), (partner, me ^ 1)):
        from_left = shifted(base, 2)
        from_right = shifted(base, -2)
        if origin is not me:
            from_left, tables = lax.optimization_barrier((from_left, tables))
        far = jnp.concatenate(
            [shifted(from_left[..., :half], 2), shifted(from_right[..., half:], -2)], axis=-1
        )
        pieces += [base, from_left, from_right, far]
        owners += [origin, (origin - 2) % count, (origin + 2) % count, (origin + 4) % count]
    return jnp.concatenate(pieces, axis=0), tables


def space_halo(edge_last, edge_first):
    count = lax.axis_size("space")
    up = [(i, i + 1) for i in range(count - 1)]
    down = [(i + 1, i) for i in range(count - 1)]
    return lax.ppermute(edge_last, "space", up), lax.ppermute(edge_first, "space", down)


def local(modes, kl_fields, triples, ratios, mode_of_slot):
    groups = lax.axis_size("chaos")
    own_modes = modes.shape[0]
    mode_count = own_modes * groups
    kl_terms = kl_fields.shape[0]
    rows = modes.shape[1]
    me = lax.axis_index("chaos")
    order = jnp.stack(
        [me, (me - 2) % groups, (me + 2) % groups, (me + 4) % groups,
         me ^ 1, ((me ^ 1) - 2) % groups, ((me ^ 1) + 2) % groups, ((me ^ 1) + 4) % groups]
    ).astype(jnp.int32)

    slot_ids = jnp.arange(mode_count, dtype=jnp.int32)
    slot_of_mode = jnp.sum(jnp.where(mode_of_slot[None, :] == slot_ids[:, None], slot_ids[None, :], 0), axis=1)
    owner_at = jnp.argmax(order[None, :] == jnp.arange(groups, dtype=jnp.int32)[:, None], axis=1).astype(jnp.int32)
    place_of_mode = owner_at[slot_of_mode // own_modes] * own_modes + slot_of_mode % own_modes
    partner_place = jnp.sum(
        jnp.where(triples[:, 1:2] == slot_ids[None, :], place_of_mode[None, :], 0), axis=1
    )
    row_weight = ratios[:, 0].astype(jnp.float32) / ratios[:, 1].astype(jnp.float32)
    local_modes = lax.dynamic_slice_in_dim(mode_of_slot, me * own_modes, own_modes)
    row_count = triples.shape[0]
    hit = (triples[None, None, :, 0] == local_modes[:, None, None]) & (
        triples[None, None, :, 2] == jnp.arange(kl_terms, dtype=jnp.int32)[None, :, None]
    )
    row_ids = jnp.arange(row_count, dtype=jnp.int32)
    t0 = jnp.argmax(hit, axis=-1).astype(jnp.int32)
    is_first = hit & (row_ids == t0[..., None])
    is_other = hit & (row_ids != t0[..., None])
    w_first = jnp.sum(jnp.where(is_first, row_weight, 0.0), axis=-1)
    w_last = jnp.sum(jnp.where(is_other, row_weight, 0.0), axis=-1)
    first = jnp.sum(jnp.where(is_first, partner_place, 0), axis=-1)
    last = jnp.sum(jnp.where(is_other, partner_place, 0), axis=-1)
    weights = jnp.stack([w_first, w_last], axis=-1).reshape(own_modes, 2 * kl_terms)
    partners = jnp.stack([first, last], axis=-1).reshape(own_modes, 2 * kl_terms)

    above, below = space_halo(kl_fields[:, rows - 1:], kl_fields[:, :1])
    coef = jnp.concatenate([above, kl_fields, below], axis=1)

    every, tables = ring_gather(modes, (partners, weights, coef))
    partners, weights, coef = tables
    applied, to_prev, to_next = stencil_apply(every, coef, partners, weights)

    from_prev, from_next = space_halo(to_next, to_prev)
    row = lax.broadcasted_iota(jnp.int32, applied.shape, 1)
    rim = jnp.where(row == 0, from_prev[:, None], jnp.where(row == rows - 1, from_next[:, None], 0.0))
    return applied - rim


def stencil_kernel(partners, weights, every, coef, out, to_prev, to_next, edges):
    slot = pl.program_id(0)
    kl_terms = coef.shape[0]
    rows = out.shape[1]
    cols = out.shape[2]

    @pl.when(slot == 0)
    def _():
        row = lax.broadcasted_iota(jnp.int32, (rows, cols), 0)
        column = lax.broadcasted_iota(jnp.int32, (rows, cols), 1)
        zero = jnp.zeros((rows, cols), jnp.float32)
        for k in range(kl_terms):
            a_c = coef[k, pl.ds(1, rows), :]
            c_up = 0.5 * (a_c + coef[k, pl.ds(0, rows), :])
            c_dn = 0.5 * (a_c + coef[k, pl.ds(2, rows), :])
            c_lf = 0.5 * (a_c + jnp.where(column == 0, zero, pltpu.roll(a_c, 1, 1)))
            c_rt = 0.5 * (a_c + jnp.where(column == cols - 1, zero, pltpu.roll(a_c, cols - 1, 1)))
            edges[0, k] = (c_up + c_dn) + (c_lf + c_rt)
            edges[1, k] = jnp.where(row == 0, zero, c_up)
            edges[2, k] = jnp.where(row == rows - 1, zero, c_dn)
            edges[3, k] = jnp.where(column == 0, zero, c_lf)
            edges[4, k] = jnp.where(column == cols - 1, zero, c_rt)
            edges[5, k] = jnp.where(row == 0, c_up, jnp.where(row == rows - 1, c_dn, zero))

    acc = jnp.zeros((rows, cols), jnp.float32)
    rim = jnp.zeros((rows, cols), jnp.float32)
    for k in range(kl_terms):
        j0 = partners[slot, 2 * k]
        j1 = partners[slot, 2 * k + 1]
        w0 = weights[slot, 2 * k]
        w1 = weights[slot, 2 * k + 1]
        center = w0 * every[j0] + w1 * every[j1]
        up = pltpu.roll(center, 1, 0)
        dn = pltpu.roll(center, rows - 1, 0)
        lf = pltpu.roll(center, 1, 1)
        rt = pltpu.roll(center, cols - 1, 1)
        term = edges[0, k] * center - edges[1, k] * up
        term = term - edges[2, k] * dn
        term = term - edges[3, k] * lf
        term = term - edges[4, k] * rt
        acc = acc + term
        rim = rim + edges[5, k] * center
    out[0] = acc
    to_prev[pl.ds(slot, 1), :] = rim[0:1]
    to_next[pl.ds(slot, 1), :] = rim[rows - 1:rows]


def stencil_apply(every, coef, partners, weights):
    own_modes = partners.shape[0]
    kl_terms = coef.shape[0]
    rows = every.shape[1]
    cols = every.shape[2]
    return pl.pallas_call(
        stencil_kernel,
        out_shape=(
            jax.ShapeDtypeStruct((own_modes, rows, cols), jnp.float32),
            jax.ShapeDtypeStruct((own_modes, cols), jnp.float32),
            jax.ShapeDtypeStruct((own_modes, cols), jnp.float32),
        ),
        grid_spec=pltpu.PrefetchScalarGridSpec(
            num_scalar_prefetch=1,
            grid=(own_modes,),
            in_specs=[
                pl.BlockSpec(memory_space=pltpu.SMEM),
                pl.BlockSpec(memory_space=pltpu.VMEM),
                pl.BlockSpec(memory_space=pltpu.VMEM),
            ],
            out_specs=(
                pl.BlockSpec((1, rows, cols), lambda i, p: (i, 0, 0)),
                pl.BlockSpec(memory_space=pltpu.VMEM),
                pl.BlockSpec(memory_space=pltpu.VMEM),
            ),
            scratch_shapes=[pltpu.VMEM((6, kl_terms, rows, cols), jnp.float32)],
        ),
        compiler_params=pltpu.CompilerParams(
            dimension_semantics=("arbitrary",), vmem_limit_bytes=48 * 1024 * 1024
        ),
    )(partners, weights, every, coef)


def solution(mesh):
    return jax.shard_map(
        local,
        mesh=mesh,
        in_specs=(P("chaos", "space", None), P(None, "space", None), P(), P(), P()),
        out_specs=P("chaos", "space", None),
        check_vma=False,
    )
```

```python
import jax
import jax.numpy as jnp
from jax import lax
from jax.experimental import pallas as pl
from jax.experimental.pallas import tpu as pltpu
from jax.sharding import PartitionSpec as P


def shift_cols(x, direction):
    zero = jnp.zeros_like(x[..., :1])
    if direction > 0:
        return jnp.concatenate([zero, x[..., :-1]], axis=-1)
    return jnp.concatenate([x[..., 1:], zero], axis=-1)


def shifted(x, step):
    count = lax.axis_size("chaos")
    return lax.ppermute(x, "chaos", [(c, (c + step) % count) for c in range(count)])


def ring_gather(block, tables):
    count = lax.axis_size("chaos")
    me = lax.axis_index("chaos")
    half = block.shape[-1] // 2
    partner = lax.ppermute(block, "chaos", [(c, c ^ 1) for c in range(count)])
    pieces = []
    owners = []
    for base, origin in ((block, me), (partner, me ^ 1)):
        from_left = shifted(base, 2)
        from_right = shifted(base, -2)
        if origin is not me:
            from_left, tables = lax.optimization_barrier((from_left, tables))
        far = jnp.concatenate(
            [shifted(from_left[..., :half], 2), shifted(from_right[..., half:], -2)], axis=-1
        )
        pieces += [base, from_left, from_right, far]
        owners += [origin, (origin - 2) % count, (origin + 2) % count, (origin + 4) % count]
    return pieces, tables


def space_halo(edge_last, edge_first):
    count = lax.axis_size("space")
    up = [(i, i + 1) for i in range(count - 1)]
    down = [(i + 1, i) for i in range(count - 1)]
    return lax.ppermute(edge_last, "space", up), lax.ppermute(edge_first, "space", down)


def local(modes, kl_fields, triples, ratios, mode_of_slot):
    groups = lax.axis_size("chaos")
    own_modes = modes.shape[0]
    mode_count = own_modes * groups
    kl_terms = kl_fields.shape[0]
    rows = modes.shape[1]
    me = lax.axis_index("chaos")
    order = jnp.stack(
        [me, (me - 2) % groups, (me + 2) % groups, (me + 4) % groups,
         me ^ 1, ((me ^ 1) - 2) % groups, ((me ^ 1) + 2) % groups, ((me ^ 1) + 4) % groups]
    ).astype(jnp.int32)

    slot_ids = jnp.arange(mode_count, dtype=jnp.int32)
    slot_of_mode = jnp.sum(jnp.where(mode_of_slot[None, :] == slot_ids[:, None], slot_ids[None, :], 0), axis=1)
    owner_at = jnp.argmax(order[None, :] == jnp.arange(groups, dtype=jnp.int32)[:, None], axis=1).astype(jnp.int32)
    place_of_mode = owner_at[slot_of_mode // own_modes] * own_modes + slot_of_mode % own_modes
    partner_place = jnp.sum(
        jnp.where(triples[:, 1:2] == slot_ids[None, :], place_of_mode[None, :], 0), axis=1
    )
    row_weight = ratios[:, 0].astype(jnp.float32) / ratios[:, 1].astype(jnp.float32)
    local_modes = lax.dynamic_slice_in_dim(mode_of_slot, me * own_modes, own_modes)
    row_count = triples.shape[0]
    hit = (triples[None, None, :, 0] == local_modes[:, None, None]) & (
        triples[None, None, :, 2] == jnp.arange(kl_terms, dtype=jnp.int32)[None, :, None]
    )
    row_ids = jnp.arange(row_count, dtype=jnp.int32)
    t0 = jnp.argmax(hit, axis=-1).astype(jnp.int32)
    is_first = hit & (row_ids == t0[..., None])
    is_other = hit & (row_ids != t0[..., None])
    w_first = jnp.sum(jnp.where(is_first, row_weight, 0.0), axis=-1)
    w_last = jnp.sum(jnp.where(is_other, row_weight, 0.0), axis=-1)
    first = jnp.sum(jnp.where(is_first, partner_place, 0), axis=-1)
    last = jnp.sum(jnp.where(is_other, partner_place, 0), axis=-1)
    weights = jnp.stack([w_first, w_last], axis=-1).reshape(own_modes, 2 * kl_terms)
    partners = jnp.stack([first, last], axis=-1).reshape(own_modes, 2 * kl_terms)

    above, below = space_halo(kl_fields[:, rows - 1:], kl_fields[:, :1])
    coef = jnp.concatenate([above, kl_fields, below], axis=1)

    early = (groups - 1) * own_modes
    late_a = partners >= early
    partners_a = jnp.where(late_a, 0, partners)
    weights_a = jnp.where(late_a, 0.0, weights)
    partners_b = jnp.where(late_a, partners - early, 0)
    weights_b = jnp.where(late_a, weights, 0.0)
    pair_b = weights_b.reshape(own_modes * kl_terms, 2)
    active = jnp.any(pair_b != 0.0, axis=1)
    rank = jnp.cumsum(active.astype(jnp.int32)) - 1
    pair_ids = jnp.arange(own_modes * kl_terms, dtype=jnp.int32)
    pick = active[None, :] & (rank[None, :] == pair_ids[:, None])
    b_pair = jnp.sum(jnp.where(pick, pair_ids[None, :], 0), axis=1)
    b_count = jnp.sum(active.astype(jnp.int32)).reshape(1)
    b_index = jnp.sum(jnp.where(pick[:, :, None], partners_b.reshape(-1, 2)[None], 0), axis=1)
    b_weight = jnp.sum(jnp.where(pick[:, :, None], pair_b[None], 0.0), axis=1)

    pieces, tables = ring_gather(modes, (partners_a, weights_a, coef, b_pair, b_count, b_index, b_weight))
    partners_a, weights_a, coef, b_pair, b_count, b_index, b_weight = tables
    every = jnp.concatenate(pieces[:-1], axis=0)
    applied, to_prev, to_next = stencil_apply(every, coef, partners_a, weights_a)
    applied, to_prev, to_next = late_apply(
        pieces[-1], coef, b_count, b_pair, b_index, b_weight, applied, to_prev, to_next
    )

    from_prev, from_next = space_halo(to_next, to_prev)
    row = lax.broadcasted_iota(jnp.int32, applied.shape, 1)
    rim = jnp.where(row == 0, from_prev[:, None], jnp.where(row == rows - 1, from_next[:, None], 0.0))
    return applied - rim


def stencil_kernel(partners, weights, every, coef, out, to_prev, to_next, edges):
    slot = pl.program_id(0)
    kl_terms = coef.shape[0]
    rows = out.shape[1]
    cols = out.shape[2]

    @pl.when(slot == 0)
    def _():
        row = lax.broadcasted_iota(jnp.int32, (rows, cols), 0)
        column = lax.broadcasted_iota(jnp.int32, (rows, cols), 1)
        zero = jnp.zeros((rows, cols), jnp.float32)
        for k in range(kl_terms):
            a_c = coef[k, pl.ds(1, rows), :]
            c_up = 0.5 * (a_c + coef[k, pl.ds(0, rows), :])
            c_dn = 0.5 * (a_c + coef[k, pl.ds(2, rows), :])
            c_lf = 0.5 * (a_c + jnp.where(column == 0, zero, pltpu.roll(a_c, 1, 1)))
            c_rt = 0.5 * (a_c + jnp.where(column == cols - 1, zero, pltpu.roll(a_c, cols - 1, 1)))
            edges[0, k] = (c_up + c_dn) + (c_lf + c_rt)
            edges[1, k] = jnp.where(row == 0, zero, c_up)
            edges[2, k] = jnp.where(row == rows - 1, zero, c_dn)
            edges[3, k] = jnp.where(column == 0, zero, c_lf)
            edges[4, k] = jnp.where(column == cols - 1, zero, c_rt)
            edges[5, k] = jnp.where(row == 0, c_up, jnp.where(row == rows - 1, c_dn, zero))

    acc = jnp.zeros((rows, cols), jnp.float32)
    rim = jnp.zeros((rows, cols), jnp.float32)
    for k in range(kl_terms):
        j0 = partners[slot, 2 * k]
        j1 = partners[slot, 2 * k + 1]
        w0 = weights[slot, 2 * k]
        w1 = weights[slot, 2 * k + 1]
        center = w0 * every[j0] + w1 * every[j1]
        up = pltpu.roll(center, 1, 0)
        dn = pltpu.roll(center, rows - 1, 0)
        lf = pltpu.roll(center, 1, 1)
        rt = pltpu.roll(center, cols - 1, 1)
        term = edges[0, k] * center - edges[1, k] * up
        term = term - edges[2, k] * dn
        term = term - edges[3, k] * lf
        term = term - edges[4, k] * rt
        acc = acc + term
        rim = rim + edges[5, k] * center
    out[0] = acc
    to_prev[pl.ds(slot, 1), :] = rim[0:1]
    to_next[pl.ds(slot, 1), :] = rim[rows - 1:rows]


def stencil_apply(every, coef, partners, weights):
    own_modes = partners.shape[0]
    kl_terms = coef.shape[0]
    rows = every.shape[1]
    cols = every.shape[2]
    return pl.pallas_call(
        stencil_kernel,
        out_shape=(
            jax.ShapeDtypeStruct((own_modes, rows, cols), jnp.float32),
            jax.ShapeDtypeStruct((own_modes, cols), jnp.float32),
            jax.ShapeDtypeStruct((own_modes, cols), jnp.float32),
        ),
        grid_spec=pltpu.PrefetchScalarGridSpec(
            num_scalar_prefetch=1,
            grid=(own_modes,),
            in_specs=[
                pl.BlockSpec(memory_space=pltpu.SMEM),
                pl.BlockSpec(memory_space=pltpu.VMEM),
                pl.BlockSpec(memory_space=pltpu.VMEM),
            ],
            out_specs=(
                pl.BlockSpec((1, rows, cols), lambda i, p: (i, 0, 0)),
                pl.BlockSpec(memory_space=pltpu.VMEM),
                pl.BlockSpec(memory_space=pltpu.VMEM),
            ),
            scratch_shapes=[pltpu.VMEM((6, kl_terms, rows, cols), jnp.float32)],
        ),
        compiler_params=pltpu.CompilerParams(
            dimension_semantics=("arbitrary",), vmem_limit_bytes=48 * 1024 * 1024
        ),
    )(partners, weights, every, coef)


def late_kernel(count, pair, index, weight, last, coef, applied, prev_in, next_in, out, to_prev, to_next, edges):
    kl_terms = coef.shape[0]
    rows = out.shape[1]
    cols = out.shape[2]
    row = lax.broadcasted_iota(jnp.int32, (rows, cols), 0)
    column = lax.broadcasted_iota(jnp.int32, (rows, cols), 1)
    zero = jnp.zeros((rows, cols), jnp.float32)
    for k in range(kl_terms):
        a_c = coef[k, pl.ds(1, rows), :]
        c_up = 0.5 * (a_c + coef[k, pl.ds(0, rows), :])
        c_dn = 0.5 * (a_c + coef[k, pl.ds(2, rows), :])
        c_lf = 0.5 * (a_c + jnp.where(column == 0, zero, pltpu.roll(a_c, 1, 1)))
        c_rt = 0.5 * (a_c + jnp.where(column == cols - 1, zero, pltpu.roll(a_c, cols - 1, 1)))
        edges[0, k] = (c_up + c_dn) + (c_lf + c_rt)
        edges[1, k] = jnp.where(row == 0, zero, c_up)
        edges[2, k] = jnp.where(row == rows - 1, zero, c_dn)
        edges[3, k] = jnp.where(column == 0, zero, c_lf)
        edges[4, k] = jnp.where(column == cols - 1, zero, c_rt)
        edges[5, k] = jnp.where(row == 0, c_up, jnp.where(row == rows - 1, c_dn, zero))
    out[...] = applied[...]
    to_prev[...] = prev_in[...]
    to_next[...] = next_in[...]

    def one_pair(r, carry):
        q = pair[r]
        slot = q // kl_terms
        k = q % kl_terms
        center = weight[r, 0] * last[index[r, 0]] + weight[r, 1] * last[index[r, 1]]
        up = pltpu.roll(center, 1, 0)
        dn = pltpu.roll(center, rows - 1, 0)
        lf = pltpu.roll(center, 1, 1)
        rt = pltpu.roll(center, cols - 1, 1)
        term = edges[0, k] * center - edges[1, k] * up
        term = term - edges[2, k] * dn
        term = term - edges[3, k] * lf
        term = term - edges[4, k] * rt
        out[slot] = out[slot] + term
        rim = edges[5, k] * center
        to_prev[pl.ds(slot, 1), :] = to_prev[pl.ds(slot, 1), :] + rim[0:1]
        to_next[pl.ds(slot, 1), :] = to_next[pl.ds(slot, 1), :] + rim[rows - 1:rows]
        return carry

    lax.fori_loop(0, count[0], one_pair, 0)


def late_apply(last, coef, count, pair, index, weight, applied, to_prev, to_next):
    own_modes, rows, cols = applied.shape
    kl_terms = coef.shape[0]
    smem = pl.BlockSpec(memory_space=pltpu.SMEM)
    vmem = pl.BlockSpec(memory_space=pltpu.VMEM)
    return pl.pallas_call(
        late_kernel,
        out_shape=(
            jax.ShapeDtypeStruct(applied.shape, jnp.float32),
            jax.ShapeDtypeStruct(to_prev.shape, jnp.float32),
            jax.ShapeDtypeStruct(to_next.shape, jnp.float32),
        ),
        in_specs=[smem, smem, smem, smem, vmem, vmem, vmem, vmem, vmem],
        out_specs=(vmem, vmem, vmem),
        scratch_shapes=[pltpu.VMEM((6, kl_terms, rows, cols), jnp.float32)],
        input_output_aliases={6: 0, 7: 1, 8: 2},
        compiler_params=pltpu.CompilerParams(vmem_limit_bytes=48 * 1024 * 1024),
    )(count, pair, index, weight, last, coef, applied, to_prev, to_next)


def solution(mesh):
    return jax.shard_map(
        local,
        mesh=mesh,
        in_specs=(P("chaos", "space", None), P(None, "space", None), P(), P(), P()),
        out_specs=P("chaos", "space", None),
        check_vma=False,
    )
```

```python
import jax
import jax.numpy as jnp
from jax import lax
from jax.experimental import pallas as pl
from jax.experimental.pallas import tpu as pltpu
from jax.sharding import PartitionSpec as P


def shift_cols(x, direction):
    zero = jnp.zeros_like(x[..., :1])
    if direction > 0:
        return jnp.concatenate([zero, x[..., :-1]], axis=-1)
    return jnp.concatenate([x[..., 1:], zero], axis=-1)


def shifted(x, step):
    count = lax.axis_size("chaos")
    return lax.ppermute(x, "chaos", [(c, (c + step) % count) for c in range(count)])


def ring_gather(block, tables):
    count = lax.axis_size("chaos")
    me = lax.axis_index("chaos")
    half = block.shape[-1] // 2
    partner = lax.ppermute(block, "chaos", [(c, c ^ 1) for c in range(count)])
    pieces = []
    owners = []
    for base, origin in ((block, me), (partner, me ^ 1)):
        from_left = shifted(base, 2)
        from_right = shifted(base, -2)
        if origin is not me:
            from_left, tables = lax.optimization_barrier((from_left, tables))
        far = jnp.concatenate(
            [shifted(from_left[..., :half], 2), shifted(from_right[..., half:], -2)], axis=-1
        )
        pieces += [base, from_left, from_right, far]
        owners += [origin, (origin - 2) % count, (origin + 2) % count, (origin + 4) % count]
    return jnp.concatenate(pieces, axis=0), tables


def space_halo(edge_last, edge_first):
    count = lax.axis_size("space")
    up = [(i, i + 1) for i in range(count - 1)]
    down = [(i + 1, i) for i in range(count - 1)]
    return lax.ppermute(edge_last, "space", up), lax.ppermute(edge_first, "space", down)


def local(modes, kl_fields, triples, ratios, mode_of_slot):
    groups = lax.axis_size("chaos")
    own_modes = modes.shape[0]
    mode_count = own_modes * groups
    kl_terms = kl_fields.shape[0]
    rows = modes.shape[1]
    me = lax.axis_index("chaos")
    order = jnp.stack(
        [me, (me - 2) % groups, (me + 2) % groups, (me + 4) % groups,
         me ^ 1, ((me ^ 1) - 2) % groups, ((me ^ 1) + 2) % groups, ((me ^ 1) + 4) % groups]
    ).astype(jnp.int32)

    slot_ids = jnp.arange(mode_count, dtype=jnp.int32)
    slot_of_mode = jnp.sum(jnp.where(mode_of_slot[None, :] == slot_ids[:, None], slot_ids[None, :], 0), axis=1)
    owner_at = jnp.argmax(order[None, :] == jnp.arange(groups, dtype=jnp.int32)[:, None], axis=1).astype(jnp.int32)
    place_of_mode = owner_at[slot_of_mode // own_modes] * own_modes + slot_of_mode % own_modes
    partner_place = jnp.sum(
        jnp.where(triples[:, 1:2] == slot_ids[None, :], place_of_mode[None, :], 0), axis=1
    )
    row_weight = ratios[:, 0].astype(jnp.float32) / ratios[:, 1].astype(jnp.float32)
    local_modes = lax.dynamic_slice_in_dim(mode_of_slot, me * own_modes, own_modes)
    row_count = triples.shape[0]
    hit = (triples[None, None, :, 0] == local_modes[:, None, None]) & (
        triples[None, None, :, 2] == jnp.arange(kl_terms, dtype=jnp.int32)[None, :, None]
    )
    row_ids = jnp.arange(row_count, dtype=jnp.int32)
    t0 = jnp.argmax(hit, axis=-1).astype(jnp.int32)
    is_first = hit & (row_ids == t0[..., None])
    is_other = hit & (row_ids != t0[..., None])
    w_first = jnp.sum(jnp.where(is_first, row_weight, 0.0), axis=-1)
    w_last = jnp.sum(jnp.where(is_other, row_weight, 0.0), axis=-1)
    first = jnp.sum(jnp.where(is_first, partner_place, 0), axis=-1)
    last = jnp.sum(jnp.where(is_other, partner_place, 0), axis=-1)
    weights = jnp.stack([w_first, w_last], axis=-1).reshape(own_modes, 2 * kl_terms)
    partners = jnp.stack([first, last], axis=-1).reshape(own_modes, 2 * kl_terms)

    above, below = space_halo(kl_fields[:, rows - 1:], kl_fields[:, :1])
    coef = jnp.concatenate([above, kl_fields, below], axis=1)

    every, tables = ring_gather(modes, (partners, weights, coef))
    partners, weights, coef = tables
    applied, to_prev, to_next = stencil_apply(every, coef, partners, weights)

    from_prev, from_next = space_halo(to_next, to_prev)
    row = lax.broadcasted_iota(jnp.int32, applied.shape, 1)
    rim = jnp.where(row == 0, from_prev[:, None], jnp.where(row == rows - 1, from_next[:, None], 0.0))
    return applied - rim


def stencil_kernel(partners, weights, every, coef, out, to_prev, to_next, edges):
    slot = pl.program_id(0)
    kl_terms = coef.shape[0]
    rows = out.shape[1]
    cols = out.shape[2]

    @pl.when(slot == 0)
    def _():
        row = lax.broadcasted_iota(jnp.int32, (rows, cols), 0)
        column = lax.broadcasted_iota(jnp.int32, (rows, cols), 1)
        zero = jnp.zeros((rows, cols), jnp.float32)
        for k in range(kl_terms):
            a_c = coef[k, pl.ds(1, rows), :]
            c_up = 0.5 * (a_c + coef[k, pl.ds(0, rows), :])
            c_dn = 0.5 * (a_c + coef[k, pl.ds(2, rows), :])
            c_lf = 0.5 * (a_c + jnp.where(column == 0, zero, pltpu.roll(a_c, 1, 1)))
            c_rt = 0.5 * (a_c + jnp.where(column == cols - 1, zero, pltpu.roll(a_c, cols - 1, 1)))
            edges[0, k] = (c_up + c_dn) + (c_lf + c_rt)
            edges[1, k] = jnp.where(row == 0, zero, c_up)
            edges[2, k] = jnp.where(row == rows - 1, zero, c_dn)
            edges[3, k] = jnp.where(column == 0, zero, c_lf)
            edges[4, k] = jnp.where(column == cols - 1, zero, c_rt)
            edges[5, k] = jnp.where(row == 0, c_up, jnp.where(row == rows - 1, c_dn, zero))

    group = out.shape[0]

    def one_slot(s, carry):
        slot = pl.program_id(0) * group + s
        acc, rim = stencil_slot(partners, weights, every, edges, slot, kl_terms, rows, cols)
        out[s] = acc
        to_prev[pl.ds(slot, 1), :] = rim[0:1]
        to_next[pl.ds(slot, 1), :] = rim[rows - 1:rows]
        return carry

    lax.fori_loop(0, group, one_slot, 0)


def stencil_slot(partners, weights, every, edges, slot, kl_terms, rows, cols):
    acc = jnp.zeros((rows, cols), jnp.float32)
    rim = jnp.zeros((rows, cols), jnp.float32)
    for k in range(kl_terms):
        j0 = partners[slot, 2 * k]
        j1 = partners[slot, 2 * k + 1]
        w0 = weights[slot, 2 * k]
        w1 = weights[slot, 2 * k + 1]
        center = w0 * every[j0] + w1 * every[j1]
        up = pltpu.roll(center, 1, 0)
        dn = pltpu.roll(center, rows - 1, 0)
        lf = pltpu.roll(center, 1, 1)
        rt = pltpu.roll(center, cols - 1, 1)
        term = edges[0, k] * center - edges[1, k] * up
        term = term - edges[2, k] * dn
        term = term - edges[3, k] * lf
        term = term - edges[4, k] * rt
        acc = acc + term
        rim = rim + edges[5, k] * center
    return acc, rim


def stencil_apply(every, coef, partners, weights):
    own_modes = partners.shape[0]
    group = next(g for g in (5, 3, 1) if own_modes % g == 0)
    kl_terms = coef.shape[0]
    rows = every.shape[1]
    cols = every.shape[2]
    return pl.pallas_call(
        stencil_kernel,
        out_shape=(
            jax.ShapeDtypeStruct((own_modes, rows, cols), jnp.float32),
            jax.ShapeDtypeStruct((own_modes, cols), jnp.float32),
            jax.ShapeDtypeStruct((own_modes, cols), jnp.float32),
        ),
        grid_spec=pltpu.PrefetchScalarGridSpec(
            num_scalar_prefetch=1,
            grid=(own_modes // group,),
            in_specs=[
                pl.BlockSpec(memory_space=pltpu.SMEM),
                pl.BlockSpec(memory_space=pltpu.VMEM),
                pl.BlockSpec(memory_space=pltpu.VMEM),
            ],
            out_specs=(
                pl.BlockSpec((group, rows, cols), lambda i, p: (i, 0, 0)),
                pl.BlockSpec(memory_space=pltpu.VMEM),
                pl.BlockSpec(memory_space=pltpu.VMEM),
            ),
            scratch_shapes=[pltpu.VMEM((6, kl_terms, rows, cols), jnp.float32)],
        ),
        compiler_params=pltpu.CompilerParams(
            dimension_semantics=("arbitrary",), vmem_limit_bytes=48 * 1024 * 1024
        ),
    )(partners, weights, every, coef)


def solution(mesh):
    return jax.shard_map(
        local,
        mesh=mesh,
        in_specs=(P("chaos", "space", None), P(None, "space", None), P(), P(), P()),
        out_specs=P("chaos", "space", None),
        check_vma=False,
    )
```

```python
import jax
import jax.numpy as jnp
from jax import lax
from jax.experimental import pallas as pl
from jax.experimental.pallas import tpu as pltpu
from jax.sharding import PartitionSpec as P


def shifted(x, step):
    count = lax.axis_size("chaos")
    return lax.ppermute(x, "chaos", [(c, (c + step) % count) for c in range(count)])


def ring_gather(block, tables):
    count = lax.axis_size("chaos")
    me = lax.axis_index("chaos")
    half = block.shape[-1] // 2
    own_left = shifted(block, 2)
    own_right = shifted(block, -2)
    partner = lax.ppermute(block, "chaos", [(c, c ^ 1) for c in range(count)])
    pieces = []
    for base, origin in ((block, me), (partner, me ^ 1)):
        if origin is me:
            from_left, from_right = own_left, own_right
        else:
            from_left = shifted(base, 2)
            from_right = shifted(base, -2)
        far = jnp.concatenate(
            [shifted(from_left[..., :half], 2), shifted(from_right[..., half:], -2)], axis=-1
        )
        pieces += [base, from_left, from_right, far]
    return jnp.concatenate(pieces, axis=0), tables


def space_halo(edge_last, edge_first):
    count = lax.axis_size("space")
    up = [(i, i + 1) for i in range(count - 1)]
    down = [(i + 1, i) for i in range(count - 1)]
    return lax.ppermute(edge_last, "space", up), lax.ppermute(edge_first, "space", down)


def local(modes, kl_fields, triples, ratios, mode_of_slot):
    groups = lax.axis_size("chaos")
    own_modes = modes.shape[0]
    mode_count = own_modes * groups
    kl_terms = kl_fields.shape[0]
    rows = modes.shape[1]
    me = lax.axis_index("chaos")
    order = jnp.stack(
        [me, (me - 2) % groups, (me + 2) % groups, (me + 4) % groups,
         me ^ 1, ((me ^ 1) - 2) % groups, ((me ^ 1) + 2) % groups, ((me ^ 1) + 4) % groups]
    ).astype(jnp.int32)

    slot_ids = jnp.arange(mode_count, dtype=jnp.int32)
    slot_of_mode = jnp.sum(jnp.where(mode_of_slot[None, :] == slot_ids[:, None], slot_ids[None, :], 0), axis=1)
    owner_at = jnp.argmax(order[None, :] == jnp.arange(groups, dtype=jnp.int32)[:, None], axis=1).astype(jnp.int32)
    place_of_mode = owner_at[slot_of_mode // own_modes] * own_modes + slot_of_mode % own_modes
    partner_place = jnp.sum(
        jnp.where(triples[:, 1:2] == slot_ids[None, :], place_of_mode[None, :], 0), axis=1
    )
    row_weight = ratios[:, 0].astype(jnp.float32) / ratios[:, 1].astype(jnp.float32)
    local_modes = lax.dynamic_slice_in_dim(mode_of_slot, me * own_modes, own_modes)
    row_count = triples.shape[0]
    hit = (triples[None, None, :, 0] == local_modes[:, None, None]) & (
        triples[None, None, :, 2] == jnp.arange(kl_terms, dtype=jnp.int32)[None, :, None]
    )
    row_ids = jnp.arange(row_count, dtype=jnp.int32)
    t0 = jnp.argmax(hit, axis=-1).astype(jnp.int32)
    is_first = hit & (row_ids == t0[..., None])
    is_other = hit & (row_ids != t0[..., None])
    w_first = jnp.sum(jnp.where(is_first, row_weight, 0.0), axis=-1)
    w_last = jnp.sum(jnp.where(is_other, row_weight, 0.0), axis=-1)
    first = jnp.sum(jnp.where(is_first, partner_place, 0), axis=-1)
    last = jnp.sum(jnp.where(is_other, partner_place, 0), axis=-1)
    weights = jnp.stack([w_first, w_last], axis=-1).reshape(own_modes, 2 * kl_terms)
    partners = jnp.stack([first, last], axis=-1).reshape(own_modes, 2 * kl_terms)

    above, below = space_halo(kl_fields[:, rows - 1:], kl_fields[:, :1])
    coef = jnp.concatenate([above, kl_fields, below], axis=1)

    every, tables = ring_gather(modes, (partners, weights, coef))
    partners, weights, coef = tables
    applied, to_prev, to_next = stencil_apply(every, coef, partners, weights)

    from_prev, from_next = space_halo(to_next, to_prev)
    row = lax.broadcasted_iota(jnp.int32, applied.shape, 1)
    rim = jnp.where(row == 0, from_prev[:, None], jnp.where(row == rows - 1, from_next[:, None], 0.0))
    return applied - rim


def stencil_kernel(partners, weights, every, coef, out, to_prev, to_next, edges):
    slot = pl.program_id(0)
    kl_terms = coef.shape[0]
    rows = out.shape[1]
    cols = out.shape[2]

    @pl.when(slot == 0)
    def _():
        row = lax.broadcasted_iota(jnp.int32, (rows, cols), 0)
        column = lax.broadcasted_iota(jnp.int32, (rows, cols), 1)
        zero = jnp.zeros((rows, cols), jnp.float32)
        for k in range(kl_terms):
            a_c = coef[k, pl.ds(1, rows), :]
            c_up = 0.5 * (a_c + coef[k, pl.ds(0, rows), :])
            c_dn = 0.5 * (a_c + coef[k, pl.ds(2, rows), :])
            c_lf = 0.5 * (a_c + jnp.where(column == 0, zero, pltpu.roll(a_c, 1, 1)))
            c_rt = 0.5 * (a_c + jnp.where(column == cols - 1, zero, pltpu.roll(a_c, cols - 1, 1)))
            edges[0, k] = (c_up + c_dn) + (c_lf + c_rt)
            edges[1, k] = jnp.where(row == 0, zero, c_up)
            edges[2, k] = jnp.where(row == rows - 1, zero, c_dn)
            edges[3, k] = jnp.where(column == 0, zero, c_lf)
            edges[4, k] = jnp.where(column == cols - 1, zero, c_rt)
            edges[5, k] = jnp.where(row == 0, c_up, jnp.where(row == rows - 1, c_dn, zero))

    acc = jnp.zeros((rows, cols), jnp.float32)
    rim = jnp.zeros((rows, cols), jnp.float32)
    for k in range(kl_terms):
        j0 = partners[slot, 2 * k]
        j1 = partners[slot, 2 * k + 1]
        w0 = weights[slot, 2 * k]
        w1 = weights[slot, 2 * k + 1]
        center = w0 * every[j0] + w1 * every[j1]
        up = pltpu.roll(center, 1, 0)
        dn = pltpu.roll(center, rows - 1, 0)
        lf = pltpu.roll(center, 1, 1)
        rt = pltpu.roll(center, cols - 1, 1)
        term = edges[0, k] * center - edges[1, k] * up
        term = term - edges[2, k] * dn
        term = term - edges[3, k] * lf
        term = term - edges[4, k] * rt
        acc = acc + term
        rim = rim + edges[5, k] * center
    out[0] = acc
    to_prev[pl.ds(slot, 1), :] = rim[0:1]
    to_next[pl.ds(slot, 1), :] = rim[rows - 1:rows]


def stencil_apply(every, coef, partners, weights):
    own_modes = partners.shape[0]
    kl_terms = coef.shape[0]
    rows = every.shape[1]
    cols = every.shape[2]
    return pl.pallas_call(
        stencil_kernel,
        out_shape=(
            jax.ShapeDtypeStruct((own_modes, rows, cols), jnp.float32),
            jax.ShapeDtypeStruct((own_modes, cols), jnp.float32),
            jax.ShapeDtypeStruct((own_modes, cols), jnp.float32),
        ),
        grid_spec=pltpu.PrefetchScalarGridSpec(
            num_scalar_prefetch=1,
            grid=(own_modes,),
            in_specs=[
                pl.BlockSpec(memory_space=pltpu.SMEM),
                pl.BlockSpec(memory_space=pltpu.VMEM),
                pl.BlockSpec(memory_space=pltpu.VMEM),
            ],
            out_specs=(
                pl.BlockSpec((1, rows, cols), lambda i, p: (i, 0, 0)),
                pl.BlockSpec(memory_space=pltpu.VMEM),
                pl.BlockSpec(memory_space=pltpu.VMEM),
            ),
            scratch_shapes=[pltpu.VMEM((6, kl_terms, rows, cols), jnp.float32)],
        ),
        compiler_params=pltpu.CompilerParams(
            dimension_semantics=("arbitrary",), vmem_limit_bytes=48 * 1024 * 1024
        ),
    )(partners, weights, every, coef)


def solution(mesh):
    return jax.shard_map(
        local,
        mesh=mesh,
        in_specs=(P("chaos", "space", None), P(None, "space", None), P(), P(), P()),
        out_specs=P("chaos", "space", None),
        check_vma=False,
    )
```
